32 devices in a mesh: groups: 2 (over x), shot: 16 (over z, y, core).
Axes of the slice: x: 2, y: 2, z: 4, core: 2. Of those that a mesh axis runs over, the one named last changes fastest.
Arguments:
- speed_blocks: float32 [2048, 2048], P(('groups', 'shot')), parts along dimension 0, may hold values from 0.03 to 0.09
- aniso_blocks: float32 [2048, 2048], P(('groups', 'shot')), parts along dimension 0, may hold values from 0 to 0.25
- block_owner: int32 [4096, 1], P(('groups', 'shot')), parts along dimension 0, may hold values from 0 to 15; in each aligned block of 128 rows (0 to 127, 128 to 255, ...) at most 16 rows name the same one
- block_slot: int32 [4096], P(('groups', 'shot')), parts along dimension 0, may hold values from 0 to 63
- state_now: float32 [4096, 16, 128], P(('groups', 'shot')), parts along dimension 0, may hold values from -6 to 6
- state_prev: float32 [4096, 16, 128], P(('groups', 'shot')), parts along dimension 0, may hold values from -6 to 6
- adjoint_now: float32 [4096, 16, 128], P(('groups', 'shot')), parts along dimension 0, may hold values from -6 to 6
- adjoint_prev: float32 [4096, 16, 128], P(('groups', 'shot')), parts along dimension 0, may hold values from -6 to 6
- source_cell: int32 [32], P(('groups', 'shot')), parts along dimension 0, may hold values from 0 to 262143
- wavelet: float32 [32, 4], P(('groups', 'shot')), parts along dimension 0, may hold values from -8 to 8
- receiver_cell: int32 [32, 256], P(('groups', 'shot')), parts along dimension 0, may hold values from 0 to 262143
- observed: float32 [32, 4, 256], P(('groups', 'shot')), parts along dimension 0, may hold values from -6 to 6
Outputs:
- final_wave: float32 [4096, 16, 128], P(('groups', 'shot')), parts along dimension 0
- model_gradient: float32 [2048, 2, 2048], P(('groups', 'shot')), parts along dimension 0
The draws below stay inside these ranges and needn't reach their ends.
There are 2 independent parts, one for each index of `groups`. The reference program is written for one: setup_inputs(seed, part) draws one part's arguments, and reference() takes and returns one part's arrays. A program takes and returns all parts, laid end to end along the dimension named above; each array names one. Nothing has to cross between parts.
Inputs may be any that keep to these rules, and one draw needn't show every extreme that they name: `block_owner`: among the 128 rows of one shot device no owner appears more than 16 times, and some owner appears exactly 16 times.
All inputs are finite; a program needn't handle non-finite values.
Results may differ from the reference program's by a relative error of at most 0.00017.
Values sent between devices are 32-bit elements; how exact they have to be, the bound alone decides.
No kernel may reach another device: no remote copies, remote signals or barrier semaphores. Data moves between devices by JAX's collectives and lax.ppermute only.
A program may use at most 128 MiB of HBM per device.

```python
import math
import jax
import jax.numpy as jnp
import numpy as np

NEED = 128
CY = 16
NZ = 128
STEPS = 4
NREC = 256
SPLIT = 8
BLK_DEV = 64
CAP = 16
NBLK = 1024
N_SHOT = 16


def touch_ends(entries, stream_key, least, high):
    longest = entries.shape.index(max(entries.shape))
    spots = []
    for shift in (0, 1):
        where = [jax.random.randint(jax.random.fold_in(stream_key, axis), (), 0, length) for axis, length in enumerate(entries.shape)]
        where[longest] = (where[longest] + shift) % entries.shape[longest]
        spots.append(tuple(where))
    return entries.at[spots[0]].set(least).at[spots[1]].set(high)


def block_levels(key, dims, cuts, low, top_value):
    factor_of = 1.0
    for axis_at, shards_of in cuts:
        steps = jax.random.uniform(jax.random.fold_in(jax.random.fold_in(key, 6), axis_at), (shards_of,), jnp.float32, low / len(cuts), top_value / len(cuts))
        factor_of = factor_of * jnp.repeat(jnp.exp(steps), dims[axis_at] // shards_of).reshape((-1,) + (1,) * (len(dims) - 1 - axis_at))
    return factor_of


def routed_block(rng, own, number, rows, number_of, top, most, skew):
    order = jax.random.permutation(rng, number_of)
    crowded, ordinary = portions_of(number_of, rows * top, most, skew, True), portions_of(number_of, rows * top, most, skew, False)
    places = jnp.arange(number_of)

    def named(tallies, turn):
        used = int((tallies > 0).sum())
        fixed = max(1, used // 4)
        shifted = fixed + (places - fixed + turn * (used - fixed)) % max(1, number_of - fixed)
        return jnp.zeros((number_of,), jnp.int32).at[order[jnp.where(places < fixed, places, shifted)]].set(jnp.asarray(tallies, jnp.int32))

    tallies = jnp.where(number % 4 == 0, named(crowded, number // 4), named(ordinary, number - number // 4 - 1))
    mixed = jax.random.permutation(jax.random.fold_in(own, 3), number_of)
    giver, receiver = mixed[0:number_of // 2 * 2:2], mixed[1:number_of // 2 * 2:2]
    margin = jnp.minimum(tallies[giver] - 1, most - tallies[receiver]) // 2
    margin = jnp.where((giver == order[0]) | (receiver == order[0]) | (tallies[receiver] == 0), 0, jnp.maximum(margin, 0))
    shifted = jax.random.randint(jax.random.fold_in(own, 4), (number_of // 2,), 0, 1 << 20) % (margin + 1)
    tallies = tallies.at[giver].add(-shifted).at[receiver].add(shifted)
    labels = jnp.searchsorted(jnp.cumsum(tallies), jnp.arange(rows * top), side="right").astype(jnp.int32)
    listing = labels.reshape(top, rows).T
    listing = listing[jax.random.permutation(jax.random.fold_in(own, 1), rows)]
    turn = jax.random.randint(jax.random.fold_in(own, 2), (rows, 1), 0, top)
    return jnp.take_along_axis(listing, (jnp.arange(top)[None, :] + turn) % top, axis=1)


def portions_of(amount, total, most, lean, full):
    weights = [(1 << 20) // math.isqrt(grade ** lean) + 1 for grade in range(1, amount + 1)]
    largest = most if full else min(most, max(-(-total // amount), total * weights[0] // sum(weights)))
    least = 1 if total - largest >= amount - 1 else 0
    given, spare = [largest] + [least] * (amount - 1), total - largest - least * (amount - 1)
    while spare > 0:
        candidates = [i for i in range(1, amount) if given[i] < largest] or [i for i in range(1, amount) if given[i] < most]
        mass, left = sum([weights[i] for i in candidates]), spare
        for i in candidates:
            addition = min(most - given[i], max(1, left * weights[i] // mass), spare)
            given[i] = given[i] + addition
            spare = spare - addition
    return np.array(given)


def centred(rng, dims, width, reach, split=(), held_as=jnp.bfloat16):
    array = width * jax.random.normal(rng, dims, jnp.float32)
    if split:
        array = array * block_levels(rng, dims, split, -0.22, 0.18)
    return jnp.clip(array, -reach, reach).astype(held_as)


def setup_inputs(seed: int = 0, part: int = 0) -> dict:
    key_of = jax.random.split(jax.random.key(seed), 13)
    part_splits = jax.random.split(jax.random.fold_in(key_of[12], part), 13)
    speed_blocks = jnp.clip(0.03 + 0.060000004 * jax.random.uniform(part_splits[0], (NBLK, CY * NZ), jnp.float32) ** block_levels(part_splits[0], (NBLK, CY * NZ), ((0, 16),), -0.2, 0.2), 0.03, 0.09)
    aniso_blocks = jnp.clip(0.25 * jax.random.uniform(part_splits[1], (NBLK, CY * NZ), jnp.float32) ** block_levels(part_splits[1], (NBLK, CY * NZ), ((0, 16),), -0.2, 0.2), 0.0, 0.25)
    block_owner_keys = jax.random.split(jax.random.fold_in(part_splits[2], 1), (N_SHOT * NEED) // NEED)
    block_owner_turns = jax.random.permutation(jax.random.fold_in(part_splits[2], 3), (N_SHOT * NEED) // NEED)
    block_owner = jax.vmap(lambda own, number: routed_block(jax.random.fold_in(part_splits[2], 2), own, number, NEED, N_SHOT, 1, CAP, 2))(block_owner_keys, block_owner_turns).reshape((N_SHOT * NEED, 1))
    block_slot = touch_ends(jax.random.randint(part_splits[3], (N_SHOT * NEED,), 0, BLK_DEV), jax.random.fold_in(part_splits[3], 1), 0, BLK_DEV - 1).astype(jnp.int32)
    state_now = centred(part_splits[4], (N_SHOT * NEED, CY, NZ), 1.0, 6.0, ((0, 16),), jnp.float32)
    state_prev = centred(part_splits[5], (N_SHOT * NEED, CY, NZ), 1.0, 6.0, ((0, 16),), jnp.float32)
    adjoint_now = centred(part_splits[6], (N_SHOT * NEED, CY, NZ), 1.0, 6.0, ((0, 16),), jnp.float32)
    adjoint_prev = centred(part_splits[7], (N_SHOT * NEED, CY, NZ), 1.0, 6.0, ((0, 16),), jnp.float32)
    source_cell = touch_ends(jax.random.randint(part_splits[8], (N_SHOT,), 0, NEED * CY * NZ), jax.random.fold_in(part_splits[8], 1), 0, (NEED * CY * NZ) - 1).astype(jnp.int32)
    wavelet = centred(part_splits[9], (N_SHOT, STEPS), 2.0, 8.0, ((0, 16),), jnp.float32)
    receiver_cell = touch_ends(jax.random.randint(part_splits[10], (N_SHOT, NREC), 0, NEED * CY * NZ), jax.random.fold_in(part_splits[10], 1), 0, (NEED * CY * NZ) - 1).astype(jnp.int32)
    observed = centred(part_splits[11], (N_SHOT, STEPS, NREC), 1.0, 6.0, ((0, 16),), jnp.float32)
    return {"speed_blocks": speed_blocks, "aniso_blocks": aniso_blocks, "block_owner": block_owner, "block_slot": block_slot, "state_now": state_now, "state_prev": state_prev, "adjoint_now": adjoint_now, "adjoint_prev": adjoint_prev, "source_cell": source_cell, "wavelet": wavelet, "receiver_cell": receiver_cell, "observed": observed}


EDGE_SCALE = 0.02
KAPPA_RATE = 0.15
IMAGE_GAIN = 0.03125


def pad_cross(values):
    devices = jnp.arange(N_SHOT, dtype=jnp.int32)
    position = (devices + SPLIT // 2) % SPLIT
    dims_out = (N_SHOT,) + (1,) * (values.ndim - 1)
    lower_keep = jnp.logical_and(position > 0, devices > 0).astype(values.dtype).reshape(dims_out)
    upper_keep = jnp.logical_and(position < SPLIT - 1, devices < N_SHOT - 1).astype(values.dtype).reshape(dims_out)
    lower_rim = jnp.roll(values[..., -1:, :], 1, axis=0) * lower_keep
    upper_rim = jnp.roll(values[..., :1, :], -1, axis=0) * upper_keep
    return jnp.concatenate([lower_rim, values, upper_rim], axis=-2)


def curvatures(widened):
    center = widened[..., 1:-1, :]
    along_cross = widened[..., 2:, :] + widened[..., :-2, :]
    inline_pad = [(0, 0)] * (center.ndim - 3) + [(1, 1), (0, 0), (0, 0)]
    padded_inline = jnp.pad(center, inline_pad)
    along_inline = padded_inline[..., 2:, :, :] + padded_inline[..., :-2, :, :]
    depth_pad = [(0, 0)] * (center.ndim - 1) + [(1, 1)]
    padded_depth = jnp.pad(center, depth_pad)
    along_depth = padded_depth[..., 2:] + padded_depth[..., :-2]
    horizontal = along_inline + along_cross - 4.0 * center
    vertical = along_depth - 2.0 * center
    return horizontal, vertical


def diffuse(widened):
    center = widened[..., 1:-1, :]
    inline_pad = [(0, 0)] * (center.ndim - 4) + [(1, 1), (0, 0), (0, 0), (0, 0)]
    padded_inline = jnp.pad(center, inline_pad)
    depth_pad = [(0, 0)] * (center.ndim - 1) + [(1, 1)]
    padded_depth = jnp.pad(center, depth_pad)
    beside_all = [padded_inline[..., 2:, :, :, :], padded_inline[..., :-2, :, :, :],
              widened[..., 2:, :], widened[..., :-2, :],
              padded_depth[..., 2:], padded_depth[..., :-2]]
    images = center[..., 0:2, :, :]
    speed_here = center[..., 2:3, :, :]
    totals = jnp.zeros_like(images)
    for beside in beside_all:
        contrast = (beside[..., 2:3, :, :] - speed_here) / EDGE_SCALE
        weight = beside[..., 3:4, :, :] / (1.0 + contrast * contrast)
        totals = totals + weight * (beside[..., 0:2, :, :] - images)
    return images + KAPPA_RATE * totals


def reference(speed_blocks, aniso_blocks, block_owner, block_slot, state_now, state_prev, adjoint_now, adjoint_prev, source_cell, wavelet, receiver_cell, observed):
    cell_count = NEED * CY * NZ
    grid_dims = (N_SHOT, NEED, CY, NZ)
    block_index = (block_owner[:, 0] * BLK_DEV + block_slot).astype(jnp.int32)
    speeds = speed_blocks[block_index].reshape(grid_dims)
    hfactor = 1.0 + 2.0 * aniso_blocks[block_index].reshape(grid_dims)
    devices = jnp.arange(N_SHOT, dtype=jnp.int32)
    source_flat = devices * cell_count + source_cell
    receiver_flat = (devices[:, None] * cell_count + receiver_cell).reshape(-1)
    previous = state_prev.reshape(grid_dims)
    current = state_now.reshape(grid_dims)
    saved_horizontal = []
    saved_vertical = []
    misfits = []
    for time_step in range(STEPS):
        horizontal, vertical = curvatures(pad_cross(current))
        advanced = 2.0 * current - previous + speeds * (hfactor * horizontal + vertical)
        advanced = advanced.reshape(-1).at[source_flat].add(wavelet[:, time_step]).reshape(grid_dims)
        synthetic = advanced.reshape(-1)[receiver_flat].reshape(N_SHOT, NREC)
        misfits.append(synthetic - observed[:, time_step, :])
        saved_horizontal.append(horizontal)
        saved_vertical.append(vertical)
        previous, current = current, advanced
    final_wave = current.reshape(N_SHOT * NEED, CY, NZ)
    later_adjoint = adjoint_prev.reshape(grid_dims)
    adjoint = adjoint_now.reshape(grid_dims)
    image_horizontal = jnp.zeros(grid_dims, jnp.float32)
    image_vertical = jnp.zeros(grid_dims, jnp.float32)
    for time_step in range(STEPS - 1, -1, -1):
        horizontal, vertical = curvatures(pad_cross(adjoint))
        earlier = 2.0 * adjoint - later_adjoint + speeds * (hfactor * horizontal + vertical)
        earlier = earlier.reshape(-1).at[receiver_flat].add(misfits[time_step].reshape(-1)).reshape(grid_dims)
        image_horizontal = image_horizontal + earlier * saved_horizontal[time_step]
        image_vertical = image_vertical + earlier * saved_vertical[time_step]
        later_adjoint, adjoint = adjoint, earlier
    gradient_speed = hfactor * image_horizontal + image_vertical
    gradient_aniso = 2.0 * speeds * image_horizontal
    stacked = jnp.stack([gradient_speed, gradient_aniso, speeds, jnp.ones_like(speeds)], axis=2)
    smoothed = diffuse(pad_cross(stacked))
    rows_out = smoothed.reshape(N_SHOT * NEED, 2, CY * NZ)
    summed = jax.ops.segment_sum(rows_out, block_index, num_segments=NBLK)
    return final_wave, summed * IMAGE_GAIN
```

```python
import jax
import jax.numpy as jnp
from jax import lax
from jax.sharding import PartitionSpec as P

NEED = 128
STEPS = 4
SPLIT = 8
HALO = 5
MARGIN = 8

EDGE_SCALE = 0.02
KAPPA_RATE = 0.15
IMAGE_GAIN = 0.03125

HIGH = lax.Precision.HIGHEST


def neighbour_pairs(count):
    up = [(i, i + 1) for i in range(count - 1) if (i + SPLIT // 2) % SPLIT < SPLIT - 1]
    down = [(j, i) for i, j in up]
    return up, down


def exchange(top, bottom, count):
    up, down = neighbour_pairs(count)
    from_below = lax.ppermute(top, "shot", up)
    from_above = lax.ppermute(bottom, "shot", down)
    return from_below, from_above


def widen(own, below, above):
    gap = MARGIN - HALO
    rows, _, depth = own.shape
    zeros = jnp.zeros((rows, gap, depth), own.dtype)
    return jnp.concatenate([zeros, below, own, above, zeros], axis=1)


def shift_sum(v, axis):
    pad = [(0, 0)] * v.ndim
    pad[axis] = (1, 1)
    padded = jnp.pad(v, pad)
    length = v.shape[axis]
    return lax.slice_in_dim(padded, 2, length + 2, axis=axis) + lax.slice_in_dim(padded, 0, length, axis=axis)


def curvatures(v):
    horizontal = shift_sum(v, 0) + shift_sum(v, 1) - 4.0 * v
    vertical = shift_sum(v, 2) - 2.0 * v
    return horizontal, vertical


def cell_coords(cell, cross, offset):
    x = cell // (cross * 128)
    y = (cell // 128) % cross + offset
    z = cell % 128
    return x, y, z


def add_at(field, xs, ys, zs, values):
    wide = field.shape[1]
    valid = (ys >= 0) & (ys < wide)
    ys = jnp.where(valid, ys, wide + 1024)
    return field.at[xs, ys, zs].add(values, mode="drop")


def shards(
    speed_blocks,
    aniso_blocks,
    block_owner,
    block_slot,
    state_now,
    state_prev,
    adjoint_now,
    adjoint_prev,
    source_cell,
    wavelet,
    receiver_cell,
    observed,
):
    count = lax.axis_size("shot")
    me = lax.axis_index("shot")
    capacity = 2 * NEED // count
    slots_all = count * capacity
    rows, cross, depth = state_now.shape
    row_len = cross * depth
    owned = speed_blocks.shape[0]
    nrec = receiver_cell.shape[1]

    info = jnp.concatenate(
        [
            source_cell.astype(jnp.float32),
            wavelet[0],
            receiver_cell[0].astype(jnp.float32),
        ]
    )
    info = jnp.pad(info, (0, rows * depth - info.shape[0])).reshape(rows, 1, depth)
    fields = (state_now, state_prev, adjoint_now, adjoint_prev)
    top = jnp.concatenate([f[:, cross - HALO :] for f in fields] + [info], axis=1)
    bottom = jnp.concatenate([f[:, :HALO] for f in fields] + [info], axis=1)
    from_below, from_above = exchange(top, bottom, count)

    owners = block_owner[:, 0]
    column_ids = jnp.arange(count, dtype=jnp.int32)
    onehot = (owners[:, None] == column_ids[None, :]).astype(jnp.int32)
    before_count = jnp.sum((jnp.cumsum(onehot, axis=0) - onehot) * onehot, axis=1)
    placed = owners * capacity + before_count
    requests = jnp.full((slots_all,), -1, jnp.int32).at[placed].set(block_slot)
    wanted = lax.all_to_all(
        requests.reshape(count, capacity), "shot", split_axis=0, concat_axis=0, tiled=True
    ).reshape(-1)

    owned_rows = jnp.concatenate([speed_blocks, aniso_blocks], axis=1)
    pick = (wanted[:, None] == jnp.arange(owned, dtype=jnp.int32)[None, :]).astype(jnp.float32)
    outgoing = jnp.dot(pick, owned_rows, precision=HIGH)
    incoming = lax.all_to_all(
        outgoing.reshape(count, capacity, 2 * row_len),
        "shot",
        split_axis=0,
        concat_axis=0,
        tiled=True,
    ).reshape(slots_all, 2 * row_len)
    place_hot = (placed[:, None] == jnp.arange(slots_all, dtype=jnp.int32)[None, :]).astype(
        jnp.float32
    )
    fetched = jnp.dot(place_hot, incoming, precision=HIGH)
    speed_own = fetched[:, :row_len].reshape(rows, cross, depth)
    aniso_own = fetched[:, row_len:].reshape(rows, cross, depth)

    model_below, model_above = exchange(
        jnp.concatenate([speed_own[:, cross - HALO :], aniso_own[:, cross - HALO :]], axis=1),
        jnp.concatenate([speed_own[:, :HALO], aniso_own[:, :HALO]], axis=1),
        count,
    )
    speeds = widen(speed_own, model_below[:, :HALO], model_above[:, :HALO])
    hfactor = 1.0 + 2.0 * widen(aniso_own, model_below[:, HALO:], model_above[:, HALO:])

    def part(received, k):
        return received[:, k * HALO : (k + 1) * HALO]

    wide_fields = [widen(f, part(from_below, k), part(from_above, k)) for k, f in enumerate(fields)]
    info_below = from_below[:, 4 * HALO].reshape(-1)
    info_above = from_above[:, 4 * HALO].reshape(-1)

    def unpack(flat):
        src = flat[0].astype(jnp.int32)
        wav = flat[1 : 1 + STEPS]
        rec = flat[1 + STEPS : 1 + STEPS + nrec].astype(jnp.int32)
        return src, wav, rec

    src_below, wav_below, rec_below = unpack(info_below)
    src_above, wav_above, rec_above = unpack(info_above)

    lower_offset = MARGIN - cross
    upper_offset = MARGIN + cross
    sx, sy, sz = [
        jnp.stack(parts)
        for parts in zip(
            cell_coords(source_cell[0], cross, MARGIN),
            cell_coords(src_below, cross, lower_offset),
            cell_coords(src_above, cross, upper_offset),
        )
    ]
    wav_all = jnp.stack([wavelet[0], wav_below, wav_above], axis=1)
    rx_own, ry_own, rz_own = cell_coords(receiver_cell[0], cross, MARGIN)
    rx, ry, rz = [
        jnp.concatenate(parts)
        for parts in zip(
            (rx_own, ry_own, rz_own),
            cell_coords(rec_below, cross, lower_offset),
            cell_coords(rec_above, cross, upper_offset),
        )
    ]

    previous, current, later_adjoint, adjoint = wide_fields[1], wide_fields[0], wide_fields[3], wide_fields[2]
    waves = []
    misfits = []
    for time_step in range(STEPS):
        horizontal, vertical = curvatures(current)
        advanced = 2.0 * current - previous + speeds * (hfactor * horizontal + vertical)
        advanced = add_at(advanced, sx, sy, sz, wav_all[time_step])
        synthetic = advanced[rx_own, ry_own, rz_own]
        misfits.append(synthetic - observed[0, time_step])
        waves.append(current)
        previous, current = current, advanced
    final_wave = current[:, MARGIN : MARGIN + cross]

    misfit_own = jnp.stack(misfits)
    mis_below, mis_above = exchange(misfit_own, misfit_own, count)

    image_horizontal = jnp.zeros_like(current)
    image_vertical = jnp.zeros_like(current)
    for time_step in range(STEPS - 1, -1, -1):
        horizontal, vertical = curvatures(adjoint)
        earlier = 2.0 * adjoint - later_adjoint + speeds * (hfactor * horizontal + vertical)
        injected = jnp.concatenate(
            [misfit_own[time_step], mis_below[time_step], mis_above[time_step]]
        )
        earlier = add_at(earlier, rx, ry, rz, injected)
        wave_horizontal, wave_vertical = curvatures(waves[time_step])
        image_horizontal = image_horizontal + earlier * wave_horizontal
        image_vertical = image_vertical + earlier * wave_vertical
        later_adjoint, adjoint = adjoint, earlier

    gradient_speed = hfactor * image_horizontal + image_vertical
    gradient_aniso = 2.0 * speeds * image_horizontal

    position = (me + SPLIT // 2) % SPLIT
    has_below = jnp.logical_and(position > 0, me > 0).astype(jnp.float32)
    has_above = jnp.logical_and(position < SPLIT - 1, me < count - 1).astype(jnp.float32)
    wide = speeds.shape[1]
    layer = lax.broadcasted_iota(jnp.int32, (1, wide, 1), 1)
    exists = jnp.where(
        layer < MARGIN, has_below, jnp.where(layer >= MARGIN + cross, has_above, 1.0)
    )
    exists = jnp.broadcast_to(exists, speeds.shape)

    lo, hi = MARGIN, MARGIN + cross
    grads = jnp.stack([gradient_speed, gradient_aniso])
    center_g = grads[:, :, lo:hi]
    center_s = speeds[:, lo:hi]

    def neighbour(v, axis, step):
        nd = v.ndim
        ax = nd - 3 + axis
        if axis == 1:
            return lax.slice_in_dim(v, lo + step, hi + step, axis=ax)
        center = lax.slice_in_dim(v, lo, hi, axis=nd - 2)
        pad = [(0, 0)] * nd
        pad[ax] = (1, 1)
        padded = jnp.pad(center, pad)
        length = center.shape[ax]
        return lax.slice_in_dim(padded, 1 + step, 1 + step + length, axis=ax)

    totals = jnp.zeros_like(center_g)
    for axis in (0, 1, 2):
        for step in (1, -1):
            g_n = neighbour(grads, axis, step)
            s_n = neighbour(speeds, axis, step)
            e_n = neighbour(exists, axis, step)
            contrast = (s_n - center_s) / EDGE_SCALE
            weight = e_n / (1.0 + contrast * contrast)
            totals = totals + weight[None] * (g_n - center_g)
    smoothed = center_g + KAPPA_RATE * totals

    rows_out = jnp.transpose(smoothed, (1, 0, 2, 3)).reshape(rows, 2 * row_len)
    returning = jnp.dot(place_hot.T, rows_out, precision=HIGH)
    returned = lax.all_to_all(
        returning.reshape(count, capacity, 2 * row_len),
        "shot",
        split_axis=0,
        concat_axis=0,
        tiled=True,
    ).reshape(slots_all, 2 * row_len)
    summed = jnp.dot(pick.T, returned, precision=HIGH)
    return (final_wave, (summed * IMAGE_GAIN).reshape(owned, 2, row_len))


def solution(mesh):
    placed = (
        P(("groups", "shot"), None),
        P(("groups", "shot"), None),
        P(("groups", "shot"), None),
        P(("groups", "shot")),
        P(("groups", "shot"), None, None),
        P(("groups", "shot"), None, None),
        P(("groups", "shot"), None, None),
        P(("groups", "shot"), None, None),
        P(("groups", "shot")),
        P(("groups", "shot"), None),
        P(("groups", "shot"), None),
        P(("groups", "shot"), None, None),
    )
    return jax.shard_map(
        shards,
        mesh=mesh,
        in_specs=placed,
        out_specs=(P(("groups", "shot"), None, None), P(("groups", "shot"), None, None)),
        check_vma=False,
    )
```

```python
import jax
import jax.numpy as jnp
from jax import lax
from jax.sharding import PartitionSpec as P

NEED = 128
STEPS = 4
SPLIT = 8


EDGE_SCALE = 0.02
KAPPA_RATE = 0.15
IMAGE_GAIN = 0.03125


def extended(array, sides, width):
    for axis, dim in sides:
        count, length = (lax.axis_size(axis), array.shape[dim])
        up = [(i, i + 1) for i in range(count - 1) if (i + SPLIT // 2) % SPLIT < SPLIT - 1]
        down = [(j, i) for i, j in up]
        last = lax.slice_in_dim(array, length - width, length, axis=dim)
        leading = lax.slice_in_dim(array, 0, width, axis=dim)
        before = lax.ppermute(last, axis, up)
        after = lax.ppermute(leading, axis, down)
        array = jnp.concatenate([before, array, after], axis=dim)
    return array


def cross_mask(widened, axis_at):
    position = (lax.axis_index("shot") + SPLIT // 2) % SPLIT
    extent = widened.shape[axis_at]
    row_index = lax.broadcasted_iota(jnp.int32, (extent,), 0)
    keep_lower = jnp.logical_or(row_index > 0, position > 0)
    keep_upper = jnp.logical_or(row_index < extent - 1, position < SPLIT - 1)
    keep_mask = jnp.logical_and(keep_lower, keep_upper).astype(widened.dtype)
    dims_out = [1] * widened.ndim
    dims_out[axis_at] = extent
    return widened * keep_mask.reshape(dims_out)


def forward_rims(wavefield):
    return cross_mask(extended(wavefield, (("shot", 1),), 1), 1)


def adjoint_rims_of(wavefield):
    return cross_mask(extended(wavefield, (("shot", 1),), 1), 1)


def image_rims_of(stacked):
    return cross_mask(extended(stacked, (("shot", 2),), 1), 2)


def curvatures(widened):
    center = widened[..., 1:-1, :]
    along_cross = widened[..., 2:, :] + widened[..., :-2, :]
    inline_pad = [(0, 0)] * (center.ndim - 3) + [(1, 1), (0, 0), (0, 0)]
    padded_inline = jnp.pad(center, inline_pad)
    along_inline = padded_inline[..., 2:, :, :] + padded_inline[..., :-2, :, :]
    depth_pad = [(0, 0)] * (center.ndim - 1) + [(1, 1)]
    padded_depth = jnp.pad(center, depth_pad)
    along_depth = padded_depth[..., 2:] + padded_depth[..., :-2]
    horizontal = along_inline + along_cross - 4.0 * center
    vertical = along_depth - 2.0 * center
    return (horizontal, vertical)


def diffuse(widened):
    center = widened[..., 1:-1, :]
    inline_pad = [(0, 0)] * (center.ndim - 4) + [(1, 1), (0, 0), (0, 0), (0, 0)]
    padded_inline = jnp.pad(center, inline_pad)
    depth_pad = [(0, 0)] * (center.ndim - 1) + [(1, 1)]
    padded_depth = jnp.pad(center, depth_pad)
    beside_all = [
        padded_inline[..., 2:, :, :, :],
        padded_inline[..., :-2, :, :, :],
        widened[..., 2:, :],
        widened[..., :-2, :],
        padded_depth[..., 2:],
        padded_depth[..., :-2],
    ]
    images = center[..., 0:2, :, :]
    speed_here = center[..., 2:3, :, :]
    totals = jnp.zeros_like(images)
    for beside in beside_all:
        contrast = (beside[..., 2:3, :, :] - speed_here) / EDGE_SCALE
        weight = beside[..., 3:4, :, :] / (1.0 + contrast * contrast)
        totals = totals + weight * (beside[..., 0:2, :, :] - images)
    return images + KAPPA_RATE * totals


def shards(
    speed_blocks,
    aniso_blocks,
    block_owner,
    block_slot,
    state_now,
    state_prev,
    adjoint_now,
    adjoint_prev,
    source_cell,
    wavelet,
    receiver_cell,
    observed,
):
    shot_count = lax.axis_size("shot")
    capacity = 2 * NEED // shot_count
    slots_all = shot_count * capacity
    owners = block_owner[:, 0]
    column_ids = jnp.arange(shot_count, dtype=jnp.int32)
    onehot = (owners[:, None] == column_ids[None, :]).astype(jnp.int32)
    before_count = jnp.sum((jnp.cumsum(onehot, axis=0) - onehot) * onehot, axis=1)
    placed = owners * capacity + before_count
    requests = jnp.full((slots_all,), -1, jnp.int32).at[placed].set(block_slot)
    wanted = lax.all_to_all(
        requests.reshape(shot_count, capacity), "shot", split_axis=0, concat_axis=0, tiled=True
    )
    row_len = speed_blocks.shape[1]
    owned = speed_blocks.shape[0]
    wanted = wanted.reshape(-1)
    owned_rows = jnp.concatenate([speed_blocks, aniso_blocks], axis=1)
    pick = (wanted[:, None] == jnp.arange(owned, dtype=jnp.int32)[None, :]).astype(jnp.float32)
    outgoing = jnp.dot(pick, owned_rows, precision=lax.Precision.HIGHEST)
    incoming = lax.all_to_all(
        outgoing.reshape(shot_count, capacity, 2 * row_len),
        "shot",
        split_axis=0,
        concat_axis=0,
        tiled=True,
    ).reshape(slots_all, 2 * row_len)
    place_hot = (placed[:, None] == jnp.arange(slots_all, dtype=jnp.int32)[None, :]).astype(
        jnp.float32
    )
    fetched = jnp.dot(place_hot, incoming, precision=lax.Precision.HIGHEST)
    grid_dims = state_now.shape
    speeds = fetched[:, :row_len].reshape(grid_dims)
    hfactor = 1.0 + 2.0 * fetched[:, row_len:].reshape(grid_dims)
    previous = state_prev
    current = state_now
    saved_first = []
    saved_second = []
    misfits = []
    for time_step in range(STEPS):
        horizontal, vertical = curvatures(forward_rims(current))
        advanced = 2.0 * current - previous + speeds * (hfactor * horizontal + vertical)
        advanced = (
            advanced.reshape(-1).at[source_cell[0]].add(wavelet[0, time_step]).reshape(grid_dims)
        )
        synthetic = advanced.reshape(-1)[receiver_cell[0]]
        misfits.append(synthetic - observed[0, time_step])
        saved_first.append(horizontal)
        saved_second.append(vertical)
        previous, current = (current, advanced)
    later_adjoint = adjoint_prev
    adjoint = adjoint_now
    image_horizontal = jnp.zeros(grid_dims, jnp.float32)
    image_vertical = jnp.zeros(grid_dims, jnp.float32)
    for time_step in range(STEPS - 1, -1, -1):
        horizontal, vertical = curvatures(adjoint_rims_of(adjoint))
        wave_horizontal = saved_first[time_step]
        wave_vertical = saved_second[time_step]
        earlier = 2.0 * adjoint - later_adjoint + speeds * (hfactor * horizontal + vertical)
        earlier = (
            earlier.reshape(-1).at[receiver_cell[0]].add(misfits[time_step]).reshape(grid_dims)
        )
        image_horizontal = image_horizontal + earlier * wave_horizontal
        image_vertical = image_vertical + earlier * wave_vertical
        later_adjoint, adjoint = (adjoint, earlier)
    gradient_speed = hfactor * image_horizontal + image_vertical
    gradient_aniso = 2.0 * speeds * image_horizontal
    stacked = jnp.stack([gradient_speed, gradient_aniso, speeds, jnp.ones_like(speeds)], axis=1)
    smoothed = diffuse(image_rims_of(stacked))
    rows_out = smoothed.reshape(NEED, 2 * row_len)
    returning = jnp.dot(place_hot.T, rows_out, precision=lax.Precision.HIGHEST)
    returned = lax.all_to_all(
        returning.reshape(shot_count, capacity, 2 * row_len),
        "shot",
        split_axis=0,
        concat_axis=0,
        tiled=True,
    ).reshape(slots_all, 2 * row_len)
    summed = jnp.dot(pick.T, returned, precision=lax.Precision.HIGHEST)
    return (current, (summed * IMAGE_GAIN).reshape(owned, 2, row_len))


def solution(mesh):
    placed = (
        P(("groups", "shot"), None),
        P(("groups", "shot"), None),
        P(("groups", "shot"), None),
        P(("groups", "shot")),
        P(("groups", "shot"), None, None),
        P(("groups", "shot"), None, None),
        P(("groups", "shot"), None, None),
        P(("groups", "shot"), None, None),
        P(("groups", "shot")),
        P(("groups", "shot"), None),
        P(("groups", "shot"), None),
        P(("groups", "shot"), None, None),
    )
    return jax.shard_map(
        shards,
        mesh=mesh,
        in_specs=placed,
        out_specs=(P(("groups", "shot"), None, None), P(("groups", "shot"), None, None)),
        check_vma=False,
    )
```

```python
import jax
import jax.numpy as jnp
from jax import lax
from jax.sharding import PartitionSpec as P
from jax.experimental import pallas as pl
from jax.experimental.pallas import tpu as pltpu

NEED = 128
STEPS = 4
SPLIT = 8
HALO = 5
MARGIN = 8

EDGE_SCALE = 0.02
KAPPA_RATE = 0.15
IMAGE_GAIN = 0.03125

HIGH = lax.Precision.HIGHEST


def neighbour_pairs(count):
    up = [(i, i + 1) for i in range(count - 1) if (i + SPLIT // 2) % SPLIT < SPLIT - 1]
    down = [(j, i) for i, j in up]
    return up, down


def exchange(top, bottom, count):
    up, down = neighbour_pairs(count)
    from_below = lax.ppermute(top, "shot", up)
    from_above = lax.ppermute(bottom, "shot", down)
    return from_below, from_above


def widen(own, below, above):
    gap = MARGIN - HALO
    rows, _, depth = own.shape
    zeros = jnp.zeros((rows, gap, depth), own.dtype)
    return jnp.concatenate([zeros, below, own, above, zeros], axis=1)


def shift_sum(v, axis):
    pad = [(0, 0)] * v.ndim
    pad[axis] = (1, 1)
    padded = jnp.pad(v, pad)
    length = v.shape[axis]
    return lax.slice_in_dim(padded, 2, length + 2, axis=axis) + lax.slice_in_dim(padded, 0, length, axis=axis)


def curvatures(v):
    horizontal = shift_sum(v, 0) + shift_sum(v, 1) - 4.0 * v
    vertical = shift_sum(v, 2) - 2.0 * v
    return horizontal, vertical


def cell_coords(cell, cross, offset):
    x = cell // (cross * 128)
    y = (cell // 128) % cross + offset
    z = cell % 128
    return x, y, z


def add_at(field, xs, ys, zs, values):
    wide = field.shape[1]
    valid = (ys >= 0) & (ys < wide)
    ys = jnp.where(valid, ys, wide + 1024)
    return field.at[xs, ys, zs].add(values, mode="drop")


CX = 4


def stencil(c, xp, xm):
    n_y, n_z = c.shape[1], c.shape[2]
    lane = lax.broadcasted_iota(jnp.int32, c.shape, 2)
    yp = pltpu.roll(c, n_y - 1, 1)
    ym = pltpu.roll(c, 1, 1)
    zp = jnp.where(lane == n_z - 1, 0.0, pltpu.roll(c, n_z - 1, 2))
    zm = jnp.where(lane == 0, 0.0, pltpu.roll(c, 1, 2))
    horizontal = (xp + xm) + (yp + ym) - 4.0 * c
    vertical = (zp + zm) - 2.0 * c
    return horizontal, vertical


def step_pass(buf, cur, prev, new, sp, hf):
    rows = sp.shape[0]

    def body(i, carry):
        x0 = pl.multiple_of(i * CX, CX)
        c = buf[cur, pl.ds(x0 + 1, CX)]
        horizontal, vertical = stencil(c, buf[cur, pl.ds(x0 + 2, CX)], buf[cur, pl.ds(x0, CX)])
        advanced = 2.0 * c - buf[prev, pl.ds(x0 + 1, CX)] + sp[pl.ds(x0, CX)] * (
            hf[pl.ds(x0, CX)] * horizontal + vertical
        )
        buf[new, pl.ds(x0 + 1, CX)] = advanced
        return carry

    lax.fori_loop(0, rows // CX, body, 0)


def add_points(buf, slot, coords, vals, base, count):
    depth = buf.shape[-1]
    sub = lax.broadcasted_iota(jnp.int32, (8, depth), 0)
    lane = lax.broadcasted_iota(jnp.int32, (8, depth), 1)

    def body(k, carry):
        x = coords[3 * k]
        y = coords[3 * k + 1]
        z = coords[3 * k + 2]
        val = vals[base + k]
        y8 = pl.multiple_of((y // 8) * 8, 8)
        tile = buf[slot, x + 1, pl.ds(y8, 8), :]
        hit = (sub == y - y8) & (lane == z)
        buf[slot, x + 1, pl.ds(y8, 8), :] = tile + jnp.where(hit, val, 0.0)
        return carry

    lax.fori_loop(0, count, body, 0)


def load_padded(buf, slot, field):
    rows = field.shape[0]

    def body(i, carry):
        x0 = pl.multiple_of(i * CX, CX)
        buf[slot, pl.ds(x0 + 1, CX)] = field[pl.ds(x0, CX)]
        return carry

    lax.fori_loop(0, rows // CX, body, 0)


def zero_edges(buf):
    zero = jnp.zeros(buf.shape[2:], jnp.float32)
    for slot in range(buf.shape[0]):
        buf[slot, 0] = zero
        buf[slot, buf.shape[1] - 1] = zero


def run_forward(buf, slots, src_c, src_v, sp, hf, after_step, steps):
    n_src = src_c.shape[0] // 3
    for t in range(steps):
        step_pass(buf, slots[t + 1], slots[t], slots[t + 2], sp, hf)
        add_points(buf, slots[t + 2], src_c, src_v, t * n_src, n_src)
        after_step(t, slots[t + 2])


def forward_kernel(src_c, src_v, rec_c, u0, um1, sp, hf, final_out, synth_out, buf):
    zero_edges(buf)
    load_padded(buf, 0, um1)
    load_padded(buf, 1, u0)
    nrec = rec_c.shape[0] // 3
    depth = buf.shape[-1]
    sub = lax.broadcasted_iota(jnp.int32, (8, depth), 0)
    lane = lax.broadcasted_iota(jnp.int32, (8, depth), 1)

    def after_step(t, slot):
        def body(r, carry):
            x = rec_c[3 * r]
            y = rec_c[3 * r + 1]
            z = rec_c[3 * r + 2]
            y8 = pl.multiple_of((y // 8) * 8, 8)
            tile = buf[slot, x + 1, pl.ds(y8, 8), :]
            hit = (sub == y - y8) & (lane == z)
            synth_out[t * nrec + r] = jnp.sum(jnp.where(hit, tile, 0.0), axis=0, keepdims=True)
            return carry

        lax.fori_loop(0, nrec, body, 0)

    slots = [0, 1, 2, 0, 1, 2]
    run_forward(buf, slots, src_c, src_v, sp, hf, after_step, STEPS)
    rows = sp.shape[0]
    cross = final_out.shape[1]
    lo = (buf.shape[2] - cross) // 2
    last = slots[STEPS + 1]

    def body(i, carry):
        x0 = pl.multiple_of(i * CX, CX)
        final_out[pl.ds(x0, CX)] = buf[last, pl.ds(x0 + 1, CX), lo : lo + cross]
        return carry

    lax.fori_loop(0, rows // CX, body, 0)


def adjoint_kernel(
    src_c, src_v, inj_c, inj_v, u0, um1, lam5, lam6, sp, hf, gs_out, ga_out, waves, lams, img_h, img_v
):
    zero_edges(waves)
    zero_edges(lams)
    load_padded(waves, 0, um1)
    load_padded(waves, 1, u0)
    run_forward(waves, [0, 1, 2, 3, 4], src_c, src_v, sp, hf, lambda t, slot: None, STEPS - 1)
    load_padded(lams, 0, lam6)
    load_padded(lams, 1, lam5)
    rows = sp.shape[0]
    n_inj = inj_c.shape[0] // 3
    order = [0, 1, 2, 0, 1, 2]
    for k in range(STEPS):
        t = STEPS - 1 - k
        later, now, new = order[k], order[k + 1], order[k + 2]
        step_pass(lams, now, later, new, sp, hf)
        add_points(lams, new, inj_c, inj_v, t * n_inj, n_inj)
        wave = t + 1

        def body(i, carry, new=new, wave=wave, first=(k == 0)):
            x0 = pl.multiple_of(i * CX, CX)
            c = waves[wave, pl.ds(x0 + 1, CX)]
            horizontal, vertical = stencil(
                c, waves[wave, pl.ds(x0 + 2, CX)], waves[wave, pl.ds(x0, CX)]
            )
            earlier = lams[new, pl.ds(x0 + 1, CX)]
            if first:
                img_h[pl.ds(x0, CX)] = earlier * horizontal
                img_v[pl.ds(x0, CX)] = earlier * vertical
            else:
                img_h[pl.ds(x0, CX)] = img_h[pl.ds(x0, CX)] + earlier * horizontal
                img_v[pl.ds(x0, CX)] = img_v[pl.ds(x0, CX)] + earlier * vertical
            return carry

        lax.fori_loop(0, rows // CX, body, 0)

    def body(i, carry):
        x0 = pl.multiple_of(i * CX, CX)
        h = img_h[pl.ds(x0, CX)]
        gs_out[pl.ds(x0, CX)] = hf[pl.ds(x0, CX)] * h + img_v[pl.ds(x0, CX)]
        ga_out[pl.ds(x0, CX)] = 2.0 * sp[pl.ds(x0, CX)] * h
        return carry

    lax.fori_loop(0, rows // CX, body, 0)


SMEM = pl.BlockSpec(memory_space=pltpu.SMEM)
VMEM = pl.BlockSpec(memory_space=pltpu.VMEM)
PARAMS = pltpu.CompilerParams(vmem_limit_bytes=62 * 1024 * 1024)


def forward_call(src_c, src_v, rec_c, u0, um1, sp, hf):
    rows, wide, depth = u0.shape
    nrec = rec_c.shape[0] // 3
    cross = wide - 2 * MARGIN
    return pl.pallas_call(
        forward_kernel,
        out_shape=(
            jax.ShapeDtypeStruct((rows, cross, depth), jnp.float32),
            jax.ShapeDtypeStruct((STEPS * nrec, 1, depth), jnp.float32),
        ),
        in_specs=[SMEM, SMEM, SMEM] + [VMEM] * 4,
        out_specs=(VMEM, VMEM),
        scratch_shapes=[pltpu.VMEM((3, rows + 2, wide, depth), jnp.float32)],
        compiler_params=PARAMS,
        cost_estimate=pl.CostEstimate(
            flops=STEPS * 20 * rows * wide * depth,
            bytes_accessed=5 * rows * wide * depth * 4,
            transcendentals=0,
        ),
    )(src_c, src_v, rec_c, u0, um1, sp, hf)


def adjoint_call(src_c, src_v, inj_c, inj_v, u0, um1, lam5, lam6, sp, hf):
    rows, wide, depth = u0.shape
    field = jax.ShapeDtypeStruct((rows, wide, depth), jnp.float32)
    return pl.pallas_call(
        adjoint_kernel,
        out_shape=(field, field),
        in_specs=[SMEM] * 4 + [VMEM] * 6,
        out_specs=(VMEM, VMEM),
        scratch_shapes=[
            pltpu.VMEM((STEPS + 1, rows + 2, wide, depth), jnp.float32),
            pltpu.VMEM((3, rows + 2, wide, depth), jnp.float32),
            pltpu.VMEM((rows, wide, depth), jnp.float32),
            pltpu.VMEM((rows, wide, depth), jnp.float32),
        ],
        compiler_params=PARAMS,
        cost_estimate=pl.CostEstimate(
            flops=STEPS * 70 * rows * wide * depth,
            bytes_accessed=8 * rows * wide * depth * 4,
            transcendentals=0,
        ),
    )(src_c, src_v, inj_c, inj_v, u0, um1, lam5, lam6, sp, hf)


def shards(
    speed_blocks,
    aniso_blocks,
    block_owner,
    block_slot,
    state_now,
    state_prev,
    adjoint_now,
    adjoint_prev,
    source_cell,
    wavelet,
    receiver_cell,
    observed,
):
    count = lax.axis_size("shot")
    me = lax.axis_index("shot")
    capacity = 2 * NEED // count
    slots_all = count * capacity
    rows, cross, depth = state_now.shape
    row_len = cross * depth
    owned = speed_blocks.shape[0]
    nrec = receiver_cell.shape[1]

    wide_y = cross + 2 * MARGIN
    info = jnp.concatenate(
        [
            source_cell.astype(jnp.float32),
            wavelet[0],
            receiver_cell[0].astype(jnp.float32),
        ]
    )
    info = jnp.pad(info, (0, rows * depth - info.shape[0])).reshape(rows, 1, depth)
    fields = (state_now, state_prev, adjoint_now, adjoint_prev)
    top = jnp.concatenate([f[:, cross - HALO :] for f in fields] + [info], axis=1)
    bottom = jnp.concatenate([f[:, :HALO] for f in fields] + [info], axis=1)
    from_below, from_above = exchange(top, bottom, count)

    owners = block_owner[:, 0]
    column_ids = jnp.arange(count, dtype=jnp.int32)
    onehot = (owners[:, None] == column_ids[None, :]).astype(jnp.int32)
    before_count = jnp.sum((jnp.cumsum(onehot, axis=0) - onehot) * onehot, axis=1)
    placed = owners * capacity + before_count
    requests = jnp.full((slots_all,), -1, jnp.int32).at[placed].set(block_slot)
    wanted = lax.all_to_all(
        requests.reshape(count, capacity), "shot", split_axis=0, concat_axis=0, tiled=True
    ).reshape(-1)

    owned_rows = jnp.concatenate([speed_blocks, aniso_blocks], axis=1)
    pick = (wanted[:, None] == jnp.arange(owned, dtype=jnp.int32)[None, :]).astype(jnp.float32)
    outgoing = jnp.dot(pick, owned_rows, precision=HIGH)
    incoming = lax.all_to_all(
        outgoing.reshape(count, capacity, 2 * row_len),
        "shot",
        split_axis=0,
        concat_axis=0,
        tiled=True,
    ).reshape(slots_all, 2 * row_len)
    place_hot = (placed[:, None] == jnp.arange(slots_all, dtype=jnp.int32)[None, :]).astype(
        jnp.float32
    )
    fetched = jnp.dot(place_hot, incoming, precision=HIGH)
    speed_own = fetched[:, :row_len].reshape(rows, cross, depth)
    aniso_own = fetched[:, row_len:].reshape(rows, cross, depth)

    model_below, model_above = exchange(
        jnp.concatenate([speed_own[:, cross - HALO :], aniso_own[:, cross - HALO :]], axis=1),
        jnp.concatenate([speed_own[:, :HALO], aniso_own[:, :HALO]], axis=1),
        count,
    )
    speeds = widen(speed_own, model_below[:, :HALO], model_above[:, :HALO])
    hfactor = 1.0 + 2.0 * widen(aniso_own, model_below[:, HALO:], model_above[:, HALO:])

    def part(received, k):
        return received[:, k * HALO : (k + 1) * HALO]

    wide_fields = [widen(f, part(from_below, k), part(from_above, k)) for k, f in enumerate(fields)]
    info_below = from_below[:, 4 * HALO].reshape(-1)
    info_above = from_above[:, 4 * HALO].reshape(-1)

    def unpack(flat):
        src = flat[0].astype(jnp.int32)
        wav = flat[1 : 1 + STEPS]
        rec = flat[1 + STEPS : 1 + STEPS + nrec].astype(jnp.int32)
        return src, wav, rec

    src_below, wav_below, rec_below = unpack(info_below)
    src_above, wav_above, rec_above = unpack(info_above)

    lower_offset = MARGIN - cross
    upper_offset = MARGIN + cross
    sx, sy, sz = [
        jnp.stack(parts)
        for parts in zip(
            cell_coords(source_cell[0], cross, MARGIN),
            cell_coords(src_below, cross, lower_offset),
            cell_coords(src_above, cross, upper_offset),
        )
    ]
    wav_all = jnp.stack([wavelet[0], wav_below, wav_above], axis=1)
    rx_own, ry_own, rz_own = cell_coords(receiver_cell[0], cross, MARGIN)
    rx, ry, rz = [
        jnp.concatenate(parts)
        for parts in zip(
            (rx_own, ry_own, rz_own),
            cell_coords(rec_below, cross, lower_offset),
            cell_coords(rec_above, cross, upper_offset),
        )
    ]

    u_now, u_before, lam_now, lam_later = wide_fields
    valid_src = (sy >= 0) & (sy < wide_y)
    src_coords = jnp.stack([sx, jnp.where(valid_src, sy, 0), sz], axis=1).reshape(-1)
    src_vals = jnp.where(valid_src[None, :], wav_all, 0.0).reshape(-1)
    rec_coords = jnp.stack([rx_own, ry_own, rz_own], axis=1).reshape(-1)
    final_wide, synth_rows = forward_call(
        src_coords, src_vals, rec_coords, u_now, u_before, speeds, hfactor
    )
    final_wave = final_wide
    synthetic = jnp.sum(synth_rows, axis=-1).reshape(STEPS, nrec)
    misfit_own = synthetic - observed[0]
    mis_below, mis_above = exchange(misfit_own, misfit_own, count)
    valid_rec = (ry >= 0) & (ry < wide_y)
    inj_coords = jnp.stack([rx, jnp.where(valid_rec, ry, 0), rz], axis=1).reshape(-1)
    injected = jnp.concatenate([misfit_own, mis_below, mis_above], axis=1)
    inj_vals = jnp.where(valid_rec[None, :], injected, 0.0).reshape(-1)
    gradient_speed, gradient_aniso = adjoint_call(
        src_coords, src_vals, inj_coords, inj_vals, u_now, u_before, lam_now, lam_later, speeds, hfactor
    )

    position = (me + SPLIT // 2) % SPLIT
    has_below = jnp.logical_and(position > 0, me > 0).astype(jnp.float32)
    has_above = jnp.logical_and(position < SPLIT - 1, me < count - 1).astype(jnp.float32)
    wide = speeds.shape[1]
    layer = lax.broadcasted_iota(jnp.int32, (1, wide, 1), 1)
    exists = jnp.where(
        layer < MARGIN, has_below, jnp.where(layer >= MARGIN + cross, has_above, 1.0)
    )
    exists = jnp.broadcast_to(exists, speeds.shape)

    lo, hi = MARGIN, MARGIN + cross
    grads = jnp.stack([gradient_speed, gradient_aniso])
    center_g = grads[:, :, lo:hi]
    center_s = speeds[:, lo:hi]

    def neighbour(v, axis, step):
        nd = v.ndim
        ax = nd - 3 + axis
        if axis == 1:
            return lax.slice_in_dim(v, lo + step, hi + step, axis=ax)
        center = lax.slice_in_dim(v, lo, hi, axis=nd - 2)
        pad = [(0, 0)] * nd
        pad[ax] = (1, 1)
        padded = jnp.pad(center, pad)
        length = center.shape[ax]
        return lax.slice_in_dim(padded, 1 + step, 1 + step + length, axis=ax)

    totals = jnp.zeros_like(center_g)
    for axis in (0, 1, 2):
        for step in (1, -1):
            g_n = neighbour(grads, axis, step)
            s_n = neighbour(speeds, axis, step)
            e_n = neighbour(exists, axis, step)
            contrast = (s_n - center_s) / EDGE_SCALE
            weight = e_n / (1.0 + contrast * contrast)
            totals = totals + weight[None] * (g_n - center_g)
    smoothed = center_g + KAPPA_RATE * totals

    rows_out = jnp.transpose(smoothed, (1, 0, 2, 3)).reshape(rows, 2 * row_len)
    returning = jnp.dot(place_hot.T, rows_out, precision=HIGH)
    returned = lax.all_to_all(
        returning.reshape(count, capacity, 2 * row_len),
        "shot",
        split_axis=0,
        concat_axis=0,
        tiled=True,
    ).reshape(slots_all, 2 * row_len)
    summed = jnp.dot(pick.T, returned, precision=HIGH)
    return (final_wave, (summed * IMAGE_GAIN).reshape(owned, 2, row_len))


def solution(mesh):
    placed = (
        P(("groups", "shot"), None),
        P(("groups", "shot"), None),
        P(("groups", "shot"), None),
        P(("groups", "shot")),
        P(("groups", "shot"), None, None),
        P(("groups", "shot"), None, None),
        P(("groups", "shot"), None, None),
        P(("groups", "shot"), None, None),
        P(("groups", "shot")),
        P(("groups", "shot"), None),
        P(("groups", "shot"), None),
        P(("groups", "shot"), None, None),
    )
    return jax.shard_map(
        shards,
        mesh=mesh,
        in_specs=placed,
        out_specs=(P(("groups", "shot"), None, None), P(("groups", "shot"), None, None)),
        check_vma=False,
    )
```

```python
import jax
import jax.numpy as jnp
from jax import lax
from jax.sharding import PartitionSpec as P
from jax.experimental import pallas as pl
from jax.experimental.pallas import tpu as pltpu

NEED = 128
STEPS = 4
SPLIT = 8
HALO = 5
MARGIN = 8

EDGE_SCALE = 0.02
KAPPA_RATE = 0.15
IMAGE_GAIN = 0.03125

HIGH = lax.Precision.HIGHEST


def neighbour_pairs(count):
    up = [(i, i + 1) for i in range(count - 1) if (i + SPLIT // 2) % SPLIT < SPLIT - 1]
    down = [(j, i) for i, j in up]
    return up, down


def exchange(top, bottom, count):
    up, down = neighbour_pairs(count)
    from_below = lax.ppermute(top, "shot", up)
    from_above = lax.ppermute(bottom, "shot", down)
    return from_below, from_above


def widen(own, below, above):
    gap = MARGIN - HALO
    rows, _, depth = own.shape
    zeros = jnp.zeros((rows, gap, depth), own.dtype)
    return jnp.concatenate([zeros, below, own, above, zeros], axis=1)


def shift_sum(v, axis):
    pad = [(0, 0)] * v.ndim
    pad[axis] = (1, 1)
    padded = jnp.pad(v, pad)
    length = v.shape[axis]
    return lax.slice_in_dim(padded, 2, length + 2, axis=axis) + lax.slice_in_dim(padded, 0, length, axis=axis)


def curvatures(v):
    horizontal = shift_sum(v, 0) + shift_sum(v, 1) - 4.0 * v
    vertical = shift_sum(v, 2) - 2.0 * v
    return horizontal, vertical


def cell_coords(cell, cross, offset):
    x = cell // (cross * 128)
    y = (cell // 128) % cross + offset
    z = cell % 128
    return x, y, z


def add_at(field, xs, ys, zs, values):
    wide = field.shape[1]
    valid = (ys >= 0) & (ys < wide)
    ys = jnp.where(valid, ys, wide + 1024)
    return field.at[xs, ys, zs].add(values, mode="drop")


CX = 4


def stencil(c, xp, xm):
    n_y, n_z = c.shape[1], c.shape[2]
    lane = lax.broadcasted_iota(jnp.int32, c.shape, 2)
    yp = pltpu.roll(c, n_y - 1, 1)
    ym = pltpu.roll(c, 1, 1)
    zp = jnp.where(lane == n_z - 1, 0.0, pltpu.roll(c, n_z - 1, 2))
    zm = jnp.where(lane == 0, 0.0, pltpu.roll(c, 1, 2))
    horizontal = (xp + xm) + (yp + ym) - 4.0 * c
    vertical = (zp + zm) - 2.0 * c
    return horizontal, vertical


def step_pass(buf, cur, prev, new, model):
    rows = model.shape[1]
    sp, hf = model.at[0], model.at[1]

    def body(i, carry):
        x0 = pl.multiple_of(i * CX, CX)
        c = buf[cur, pl.ds(x0 + 1, CX)]
        horizontal, vertical = stencil(c, buf[cur, pl.ds(x0 + 2, CX)], buf[cur, pl.ds(x0, CX)])
        advanced = 2.0 * c - buf[prev, pl.ds(x0 + 1, CX)] + sp[pl.ds(x0, CX)] * (
            hf[pl.ds(x0, CX)] * horizontal + vertical
        )
        buf[new, pl.ds(x0 + 1, CX)] = advanced
        return carry

    lax.fori_loop(0, rows // CX, body, 0)


def add_points(buf, slot, coords, vals, base, first, count, checked):
    depth = buf.shape[-1]
    sub = lax.broadcasted_iota(jnp.int32, (8, depth), 0)
    lane = lax.broadcasted_iota(jnp.int32, (8, depth), 1)

    def one(k):
        x = coords[3 * k]
        y = coords[3 * k + 1]
        z = coords[3 * k + 2]
        val = vals[base + k]
        y8 = pl.multiple_of((y // 8) * 8, 8)
        tile = buf[slot, x + 1, pl.ds(y8, 8), :]
        hit = (sub == y - y8) & (lane == z)
        buf[slot, x + 1, pl.ds(y8, 8), :] = tile + jnp.where(hit, val, 0.0)

    def body(k, carry):
        if checked:
            pl.when(coords[3 * k + 1] > 0)(lambda: one(k))
        else:
            one(k)
        return carry

    lax.fori_loop(first, first + count, body, 0, unroll=8)


def load_padded(buf, slot, own, below, above, k, pad=1):
    rows, cross, depth = own.shape
    gap = MARGIN - HALO
    zeros = jnp.zeros((CX, gap, depth), jnp.float32)

    def body(i, carry):
        x0 = pl.multiple_of(i * CX, CX)
        xs = pl.ds(x0 + pad, CX)
        buf[slot, xs, 0:gap] = zeros
        buf[slot, xs, gap:MARGIN] = below[pl.ds(x0, CX), k * HALO : (k + 1) * HALO]
        buf[slot, xs, MARGIN : MARGIN + cross] = own[pl.ds(x0, CX)]
        buf[slot, xs, MARGIN + cross : MARGIN + cross + HALO] = above[pl.ds(x0, CX), k * HALO : (k + 1) * HALO]
        buf[slot, xs, MARGIN + cross + HALO :] = zeros
        return carry

    lax.fori_loop(0, rows // CX, body, 0)


def load_model(model, sp_own, an_own, m_lo, m_hi):
    load_padded(model, 0, sp_own, m_lo, m_hi, 0, pad=0)
    load_padded(model, 1, an_own, m_lo, m_hi, 1, pad=0)
    rows = sp_own.shape[0]

    def body(i, carry):
        x0 = pl.multiple_of(i * CX, CX)
        model[1, pl.ds(x0, CX)] = 1.0 + 2.0 * model[1, pl.ds(x0, CX)]
        return carry

    lax.fori_loop(0, rows // CX, body, 0)


def zero_edges(buf):
    zero = jnp.zeros(buf.shape[2:], jnp.float32)
    for slot in range(buf.shape[0]):
        buf[slot, 0] = zero
        buf[slot, buf.shape[1] - 1] = zero


def run_forward(buf, slots, src_c, src_v, model, after_step, steps):
    n_src = src_c.shape[0] // 3
    for t in range(steps):
        step_pass(buf, slots[t + 1], slots[t], slots[t + 2], model)
        add_points(buf, slots[t + 2], src_c, src_v, t * n_src, 0, n_src, False)
        after_step(t, slots[t + 2])


def forward_kernel(
    src_c, src_v, rec_c, u0, um1, sp_own, an_own, lo, hi, m_lo, m_hi, final_out, synth_out, buf, model
):
    zero_edges(buf)
    load_padded(buf, 0, um1, lo, hi, 1)
    load_padded(buf, 1, u0, lo, hi, 0)
    load_model(model, sp_own, an_own, m_lo, m_hi)
    nrec = rec_c.shape[0] // 3
    depth = buf.shape[-1]
    sub = lax.broadcasted_iota(jnp.int32, (8, depth), 0)
    lane = lax.broadcasted_iota(jnp.int32, (8, depth), 1)

    def after_step(t, slot):
        def body(r, carry):
            x = rec_c[3 * r]
            y = rec_c[3 * r + 1]
            z = rec_c[3 * r + 2]
            y8 = pl.multiple_of((y // 8) * 8, 8)
            tile = buf[slot, x + 1, pl.ds(y8, 8), :]
            hit = (sub == y - y8) & (lane == z)
            synth_out[t * nrec + r] = jnp.sum(jnp.where(hit, tile, 0.0), axis=0, keepdims=True)
            return carry

        lax.fori_loop(0, nrec, body, 0, unroll=8)

    slots = [0, 1, 2, 0, 1, 2]
    run_forward(buf, slots, src_c, src_v, model, after_step, STEPS)
    rows = u0.shape[0]
    cross = final_out.shape[1]
    lo = (buf.shape[2] - cross) // 2
    last = slots[STEPS + 1]

    def body(i, carry):
        x0 = pl.multiple_of(i * CX, CX)
        final_out[pl.ds(x0, CX)] = buf[last, pl.ds(x0 + 1, CX), lo : lo + cross]
        return carry

    lax.fori_loop(0, rows // CX, body, 0)


def adjoint_kernel(
    src_c, src_v, inj_c, inj_v, u0, um1, lam5, lam6, sp_own, an_own, lo, hi, m_lo, m_hi,
    gs_out, ga_out, waves, lams, img_h, img_v, model,
):
    zero_edges(waves)
    zero_edges(lams)
    load_model(model, sp_own, an_own, m_lo, m_hi)
    load_padded(waves, 0, um1, lo, hi, 1)
    load_padded(waves, 1, u0, lo, hi, 0)
    run_forward(waves, [0, 1, 2, 3, 4], src_c, src_v, model, lambda t, slot: None, STEPS - 1)
    load_padded(lams, 0, lam6, lo, hi, 3)
    load_padded(lams, 1, lam5, lo, hi, 2)
    rows = u0.shape[0]
    n_inj = inj_c.shape[0] // 3
    n_own = n_inj // 3
    order = [0, 1, 2, 0, 1, 2]
    for k in range(STEPS):
        t = STEPS - 1 - k
        later, now, new = order[k], order[k + 1], order[k + 2]
        step_pass(lams, now, later, new, model)
        add_points(lams, new, inj_c, inj_v, t * n_inj, 0, n_own, False)
        add_points(lams, new, inj_c, inj_v, t * n_inj, n_own, n_inj - n_own, True)
        wave = t + 1

        def body(i, carry, new=new, wave=wave, first=(k == 0)):
            x0 = pl.multiple_of(i * CX, CX)
            c = waves[wave, pl.ds(x0 + 1, CX)]
            horizontal, vertical = stencil(
                c, waves[wave, pl.ds(x0 + 2, CX)], waves[wave, pl.ds(x0, CX)]
            )
            earlier = lams[new, pl.ds(x0 + 1, CX)]
            if first:
                img_h[pl.ds(x0, CX)] = earlier * horizontal
                img_v[pl.ds(x0, CX)] = earlier * vertical
            else:
                img_h[pl.ds(x0, CX)] = img_h[pl.ds(x0, CX)] + earlier * horizontal
                img_v[pl.ds(x0, CX)] = img_v[pl.ds(x0, CX)] + earlier * vertical
            return carry

        lax.fori_loop(0, rows // CX, body, 0)

    def body(i, carry):
        x0 = pl.multiple_of(i * CX, CX)
        h = img_h[pl.ds(x0, CX)]
        gs_out[pl.ds(x0, CX)] = model[1, pl.ds(x0, CX)] * h + img_v[pl.ds(x0, CX)]
        ga_out[pl.ds(x0, CX)] = 2.0 * model[0, pl.ds(x0, CX)] * h
        return carry

    lax.fori_loop(0, rows // CX, body, 0)


SMEM = pl.BlockSpec(memory_space=pltpu.SMEM)
VMEM = pl.BlockSpec(memory_space=pltpu.VMEM)
PARAMS = pltpu.CompilerParams(vmem_limit_bytes=62 * 1024 * 1024)


def forward_call(src_c, src_v, rec_c, u0, um1, sp_own, an_own, lo, hi, m_lo, m_hi):
    rows, cross, depth = u0.shape
    wide = cross + 2 * MARGIN
    nrec = rec_c.shape[0] // 3
    return pl.pallas_call(
        forward_kernel,
        out_shape=(
            jax.ShapeDtypeStruct((rows, cross, depth), jnp.float32),
            jax.ShapeDtypeStruct((STEPS * nrec, 1, depth), jnp.float32),
        ),
        in_specs=[SMEM] * 3 + [VMEM] * 8,
        out_specs=(VMEM, VMEM),
        scratch_shapes=[
            pltpu.VMEM((3, rows + 2, wide, depth), jnp.float32),
            pltpu.VMEM((2, rows, wide, depth), jnp.float32),
        ],
        compiler_params=PARAMS,
        cost_estimate=pl.CostEstimate(
            flops=STEPS * 20 * rows * wide * depth,
            bytes_accessed=6 * rows * cross * depth * 4,
            transcendentals=0,
        ),
    )(src_c, src_v, rec_c, u0, um1, sp_own, an_own, lo, hi, m_lo, m_hi)


def adjoint_call(src_c, src_v, inj_c, inj_v, u0, um1, lam5, lam6, sp_own, an_own, lo, hi, m_lo, m_hi):
    rows, cross, depth = u0.shape
    wide = cross + 2 * MARGIN
    field = jax.ShapeDtypeStruct((rows, wide, depth), jnp.float32)
    return pl.pallas_call(
        adjoint_kernel,
        out_shape=(field, field),
        in_specs=[SMEM] * 4 + [VMEM] * 10,
        out_specs=(VMEM, VMEM),
        scratch_shapes=[
            pltpu.VMEM((STEPS + 1, rows + 2, wide, depth), jnp.float32),
            pltpu.VMEM((3, rows + 2, wide, depth), jnp.float32),
            pltpu.VMEM((rows, wide, depth), jnp.float32),
            pltpu.VMEM((rows, wide, depth), jnp.float32),
            pltpu.VMEM((2, rows, wide, depth), jnp.float32),
        ],
        compiler_params=PARAMS,
        cost_estimate=pl.CostEstimate(
            flops=STEPS * 70 * rows * wide * depth,
            bytes_accessed=10 * rows * cross * depth * 4,
            transcendentals=0,
        ),
    )(src_c, src_v, inj_c, inj_v, u0, um1, lam5, lam6, sp_own, an_own, lo, hi, m_lo, m_hi)


def shards(
    speed_blocks,
    aniso_blocks,
    block_owner,
    block_slot,
    state_now,
    state_prev,
    adjoint_now,
    adjoint_prev,
    source_cell,
    wavelet,
    receiver_cell,
    observed,
):
    count = lax.axis_size("shot")
    me = lax.axis_index("shot")
    capacity = 2 * NEED // count
    slots_all = count * capacity
    rows, cross, depth = state_now.shape
    row_len = cross * depth
    owned = speed_blocks.shape[0]
    nrec = receiver_cell.shape[1]

    wide_y = cross + 2 * MARGIN
    info = jnp.concatenate(
        [
            source_cell.astype(jnp.float32),
            wavelet[0],
            receiver_cell[0].astype(jnp.float32),
        ]
    )
    info = jnp.pad(info, (0, rows * depth - info.shape[0])).reshape(rows, 1, depth)
    fields = (state_now, state_prev, adjoint_now, adjoint_prev)
    top = jnp.concatenate([f[:, cross - HALO :] for f in fields] + [info], axis=1)
    bottom = jnp.concatenate([f[:, :HALO] for f in fields] + [info], axis=1)
    from_below, from_above = exchange(top, bottom, count)

    owners = block_owner[:, 0]
    column_ids = jnp.arange(count, dtype=jnp.int32)
    onehot = (owners[:, None] == column_ids[None, :]).astype(jnp.int32)
    before_count = jnp.sum((jnp.cumsum(onehot, axis=0) - onehot) * onehot, axis=1)
    placed = owners * capacity + before_count
    requests = jnp.full((slots_all,), -1, jnp.int32).at[placed].set(block_slot)
    wanted = lax.all_to_all(
        requests.reshape(count, capacity), "shot", split_axis=0, concat_axis=0, tiled=True
    ).reshape(-1)

    owned_rows = jnp.concatenate([speed_blocks, aniso_blocks], axis=1)
    pick = (wanted[:, None] == jnp.arange(owned, dtype=jnp.int32)[None, :]).astype(jnp.float32)
    outgoing = jnp.dot(pick, owned_rows, precision=HIGH)
    incoming = lax.all_to_all(
        outgoing.reshape(count, capacity, 2 * row_len),
        "shot",
        split_axis=0,
        concat_axis=0,
        tiled=True,
    ).reshape(slots_all, 2 * row_len)
    place_hot = (placed[:, None] == jnp.arange(slots_all, dtype=jnp.int32)[None, :]).astype(
        jnp.float32
    )
    fetched = jnp.dot(place_hot, incoming, precision=HIGH)
    speed_own = fetched[:, :row_len].reshape(rows, cross, depth)
    aniso_own = fetched[:, row_len:].reshape(rows, cross, depth)

    model_below, model_above = exchange(
        jnp.concatenate([speed_own[:, cross - HALO :], aniso_own[:, cross - HALO :]], axis=1),
        jnp.concatenate([speed_own[:, :HALO], aniso_own[:, :HALO]], axis=1),
        count,
    )
    info_below = from_below[:, 4 * HALO].reshape(-1)
    info_above = from_above[:, 4 * HALO].reshape(-1)

    def unpack(flat):
        src = flat[0].astype(jnp.int32)
        wav = flat[1 : 1 + STEPS]
        rec = flat[1 + STEPS : 1 + STEPS + nrec].astype(jnp.int32)
        return src, wav, rec

    src_below, wav_below, rec_below = unpack(info_below)
    src_above, wav_above, rec_above = unpack(info_above)

    lower_offset = MARGIN - cross
    upper_offset = MARGIN + cross
    sx, sy, sz = [
        jnp.stack(parts)
        for parts in zip(
            cell_coords(source_cell[0], cross, MARGIN),
            cell_coords(src_below, cross, lower_offset),
            cell_coords(src_above, cross, upper_offset),
        )
    ]
    wav_all = jnp.stack([wavelet[0], wav_below, wav_above], axis=1)
    rx_own, ry_own, rz_own = cell_coords(receiver_cell[0], cross, MARGIN)
    rx, ry, rz = [
        jnp.concatenate(parts)
        for parts in zip(
            (rx_own, ry_own, rz_own),
            cell_coords(rec_below, cross, lower_offset),
            cell_coords(rec_above, cross, upper_offset),
        )
    ]

    valid_src = (sy >= 0) & (sy < wide_y)
    src_coords = jnp.stack([sx, jnp.where(valid_src, sy, 0), sz], axis=1).reshape(-1)
    src_vals = jnp.where(valid_src[None, :], wav_all, 0.0).reshape(-1)
    rec_coords = jnp.stack([rx_own, ry_own, rz_own], axis=1).reshape(-1)
    halos = (from_below, from_above, model_below, model_above)
    final_wide, synth_rows = forward_call(
        src_coords, src_vals, rec_coords, state_now, state_prev, speed_own, aniso_own, *halos
    )
    final_wave = final_wide
    synthetic = jnp.sum(synth_rows, axis=-1).reshape(STEPS, nrec)
    misfit_own = synthetic - observed[0]
    mis_below, mis_above = exchange(misfit_own, misfit_own, count)
    valid_rec = (ry >= MARGIN - HALO + 1) & (ry < MARGIN + cross + HALO - 1)
    inj_coords = jnp.stack([rx, jnp.where(valid_rec, ry, 0), rz], axis=1).reshape(-1)
    injected = jnp.concatenate([misfit_own, mis_below, mis_above], axis=1)
    inj_vals = jnp.where(valid_rec[None, :], injected, 0.0).reshape(-1)
    gradient_speed, gradient_aniso = adjoint_call(
        src_coords, src_vals, inj_coords, inj_vals, state_now, state_prev, adjoint_now, adjoint_prev,
        speed_own, aniso_own, *halos
    )
    speeds = jnp.concatenate(
        [model_below[:, HALO - 1 : HALO], speed_own, model_above[:, 0:1]], axis=1
    )

    position = (me + SPLIT // 2) % SPLIT
    has_below = jnp.logical_and(position > 0, me > 0).astype(jnp.float32)
    has_above = jnp.logical_and(position < SPLIT - 1, me < count - 1).astype(jnp.float32)
    wide = speeds.shape[1]
    layer = lax.broadcasted_iota(jnp.int32, (1, wide, 1), 1)
    exists = jnp.where(layer < 1, has_below, jnp.where(layer >= 1 + cross, has_above, 1.0))
    exists = jnp.broadcast_to(exists, speeds.shape)

    lo, hi = 1, 1 + cross
    grads = jnp.stack([gradient_speed, gradient_aniso])[:, :, MARGIN - 1 : MARGIN + cross + 1]
    center_g = grads[:, :, lo:hi]
    center_s = speeds[:, lo:hi]

    def neighbour(v, axis, step):
        nd = v.ndim
        ax = nd - 3 + axis
        if axis == 1:
            return lax.slice_in_dim(v, lo + step, hi + step, axis=ax)
        center = lax.slice_in_dim(v, lo, hi, axis=nd - 2)
        pad = [(0, 0)] * nd
        pad[ax] = (1, 1)
        padded = jnp.pad(center, pad)
        length = center.shape[ax]
        return lax.slice_in_dim(padded, 1 + step, 1 + step + length, axis=ax)

    totals = jnp.zeros_like(center_g)
    for axis in (0, 1, 2):
        for step in (1, -1):
            g_n = neighbour(grads, axis, step)
            s_n = neighbour(speeds, axis, step)
            e_n = neighbour(exists, axis, step)
            contrast = (s_n - center_s) / EDGE_SCALE
            weight = e_n / (1.0 + contrast * contrast)
            totals = totals + weight[None] * (g_n - center_g)
    smoothed = center_g + KAPPA_RATE * totals

    rows_out = jnp.transpose(smoothed, (1, 0, 2, 3)).reshape(rows, 2 * row_len)
    returning = jnp.dot(place_hot.T, rows_out, precision=HIGH)
    returned = lax.all_to_all(
        returning.reshape(count, capacity, 2 * row_len),
        "shot",
        split_axis=0,
        concat_axis=0,
        tiled=True,
    ).reshape(slots_all, 2 * row_len)
    summed = jnp.dot(pick.T, returned, precision=HIGH)
    return (final_wave, (summed * IMAGE_GAIN).reshape(owned, 2, row_len))


def solution(mesh):
    placed = (
        P(("groups", "shot"), None),
        P(("groups", "shot"), None),
        P(("groups", "shot"), None),
        P(("groups", "shot")),
        P(("groups", "shot"), None, None),
        P(("groups", "shot"), None, None),
        P(("groups", "shot"), None, None),
        P(("groups", "shot"), None, None),
        P(("groups", "shot")),
        P(("groups", "shot"), None),
        P(("groups", "shot"), None),
        P(("groups", "shot"), None, None),
    )
    return jax.shard_map(
        shards,
        mesh=mesh,
        in_specs=placed,
        out_specs=(P(("groups", "shot"), None, None), P(("groups", "shot"), None, None)),
        check_vma=False,
    )
```

```python
import jax
import jax.numpy as jnp
from jax import lax
from jax.sharding import PartitionSpec as P
from jax.experimental import pallas as pl
from jax.experimental.pallas import tpu as pltpu

NEED = 128
STEPS = 4
SPLIT = 8
HALO = 5
MARGIN = 8

EDGE_SCALE = 0.02
KAPPA_RATE = 0.15
IMAGE_GAIN = 0.03125

HIGH = lax.Precision.HIGHEST


def neighbour_pairs(count):
    up = [(i, i + 1) for i in range(count - 1) if (i + SPLIT // 2) % SPLIT < SPLIT - 1]
    down = [(j, i) for i, j in up]
    return up, down


def exchange(top, bottom, count):
    up, down = neighbour_pairs(count)
    from_below = lax.ppermute(top, "shot", up)
    from_above = lax.ppermute(bottom, "shot", down)
    return from_below, from_above


def widen(own, below, above):
    gap = MARGIN - HALO
    rows, _, depth = own.shape
    zeros = jnp.zeros((rows, gap, depth), own.dtype)
    return jnp.concatenate([zeros, below, own, above, zeros], axis=1)


def shift_sum(v, axis):
    pad = [(0, 0)] * v.ndim
    pad[axis] = (1, 1)
    padded = jnp.pad(v, pad)
    length = v.shape[axis]
    return lax.slice_in_dim(padded, 2, length + 2, axis=axis) + lax.slice_in_dim(padded, 0, length, axis=axis)


def curvatures(v):
    horizontal = shift_sum(v, 0) + shift_sum(v, 1) - 4.0 * v
    vertical = shift_sum(v, 2) - 2.0 * v
    return horizontal, vertical


def cell_coords(cell, cross, offset):
    x = cell // (cross * 128)
    y = (cell // 128) % cross + offset
    z = cell % 128
    return x, y, z


def add_at(field, xs, ys, zs, values):
    wide = field.shape[1]
    valid = (ys >= 0) & (ys < wide)
    ys = jnp.where(valid, ys, wide + 1024)
    return field.at[xs, ys, zs].add(values, mode="drop")


CX = 4


def stencil(c, xp, xm):
    n_y, n_z = c.shape[1], c.shape[2]
    lane = lax.broadcasted_iota(jnp.int32, c.shape, 2)
    yp = pltpu.roll(c, n_y - 1, 1)
    ym = pltpu.roll(c, 1, 1)
    zp = jnp.where(lane == n_z - 1, 0.0, pltpu.roll(c, n_z - 1, 2))
    zm = jnp.where(lane == 0, 0.0, pltpu.roll(c, 1, 2))
    horizontal = (xp + xm) + (yp + ym) - 4.0 * c
    vertical = (zp + zm) - 2.0 * c
    return horizontal, vertical


def step_pass(buf, cur, prev, new, model):
    rows = model.shape[1]
    sp, hf = model.at[0], model.at[1]

    def body(i, carry):
        x0 = pl.multiple_of(i * CX, CX)
        c = buf[cur, pl.ds(x0 + 1, CX)]
        horizontal, vertical = stencil(c, buf[cur, pl.ds(x0 + 2, CX)], buf[cur, pl.ds(x0, CX)])
        advanced = 2.0 * c - buf[prev, pl.ds(x0 + 1, CX)] + sp[pl.ds(x0, CX)] * (
            hf[pl.ds(x0, CX)] * horizontal + vertical
        )
        buf[new, pl.ds(x0 + 1, CX)] = advanced
        return carry

    lax.fori_loop(0, rows // CX, body, 0)


def add_points(buf, slot, coords, vals, base, first, count):
    depth = buf.shape[-1]
    sub = lax.broadcasted_iota(jnp.int32, (8, depth), 0)
    lane = lax.broadcasted_iota(jnp.int32, (8, depth), 1)

    def one(k):
        x = coords[3 * k]
        y = coords[3 * k + 1]
        z = coords[3 * k + 2]
        val = vals[base + k]
        y8 = pl.multiple_of((y // 8) * 8, 8)
        tile = buf[slot, x + 1, pl.ds(y8, 8), :]
        hit = (sub == y - y8) & (lane == z)
        buf[slot, x + 1, pl.ds(y8, 8), :] = tile + jnp.where(hit, val, 0.0)

    def body(k, carry):
        one(k)
        return carry

    lax.fori_loop(first, first + count, body, 0)


def load_padded(buf, slot, own, below, above, k, pad=1):
    rows, cross, depth = own.shape
    gap = MARGIN - HALO
    zeros = jnp.zeros((CX, gap, depth), jnp.float32)

    def body(i, carry):
        x0 = pl.multiple_of(i * CX, CX)
        xs = pl.ds(x0 + pad, CX)
        buf[slot, xs, 0:gap] = zeros
        buf[slot, xs, gap:MARGIN] = below[pl.ds(x0, CX), k * HALO : (k + 1) * HALO]
        buf[slot, xs, MARGIN : MARGIN + cross] = own[pl.ds(x0, CX)]
        buf[slot, xs, MARGIN + cross : MARGIN + cross + HALO] = above[pl.ds(x0, CX), k * HALO : (k + 1) * HALO]
        buf[slot, xs, MARGIN + cross + HALO :] = zeros
        return carry

    lax.fori_loop(0, rows // CX, body, 0)


def load_model(model, sp_own, an_own, m_lo, m_hi):
    load_padded(model, 0, sp_own, m_lo, m_hi, 0, pad=0)
    load_padded(model, 1, an_own, m_lo, m_hi, 1, pad=0)
    rows = sp_own.shape[0]

    def body(i, carry):
        x0 = pl.multiple_of(i * CX, CX)
        model[1, pl.ds(x0, CX)] = 1.0 + 2.0 * model[1, pl.ds(x0, CX)]
        return carry

    lax.fori_loop(0, rows // CX, body, 0)


def zero_edges(buf):
    zero = jnp.zeros(buf.shape[2:], jnp.float32)
    for slot in range(buf.shape[0]):
        buf[slot, 0] = zero
        buf[slot, buf.shape[1] - 1] = zero


def run_forward(buf, slots, src_c, src_v, model, after_step, steps):
    n_src = src_c.shape[0] // 3
    for t in range(steps):
        step_pass(buf, slots[t + 1], slots[t], slots[t + 2], model)
        add_points(buf, slots[t + 2], src_c, src_v, t * n_src, 0, n_src)
        after_step(t, slots[t + 2])


def forward_kernel(src_c, src_v, u0, um1, sp_own, an_own, lo, hi, m_lo, m_hi, waves_out, buf, model):
    zero_edges(buf)
    load_padded(buf, 0, um1, lo, hi, 1)
    load_padded(buf, 1, u0, lo, hi, 0)
    load_model(model, sp_own, an_own, m_lo, m_hi)
    rows, cross = u0.shape[0], u0.shape[1]

    def after_step(t, slot):
        def body(i, carry):
            x0 = pl.multiple_of(i * CX, CX)
            waves_out[t, pl.ds(x0, CX)] = buf[slot, pl.ds(x0 + 1, CX), MARGIN : MARGIN + cross]
            return carry

        lax.fori_loop(0, rows // CX, body, 0)

    run_forward(buf, [0, 1, 2, 0, 1, 2], src_c, src_v, model, after_step, STEPS)


def adjoint_kernel(
    src_c, src_v, inj_c, inj_v, u0, um1, lam5, lam6, sp_own, an_own, lo, hi, m_lo, m_hi,
    gs_out, ga_out, waves, lams, img_h, img_v, model,
):
    zero_edges(waves)
    zero_edges(lams)
    load_model(model, sp_own, an_own, m_lo, m_hi)
    load_padded(waves, 0, um1, lo, hi, 1)
    load_padded(waves, 1, u0, lo, hi, 0)
    run_forward(waves, [0, 1, 2, 3, 4], src_c, src_v, model, lambda t, slot: None, STEPS - 1)
    load_padded(lams, 0, lam6, lo, hi, 3)
    load_padded(lams, 1, lam5, lo, hi, 2)
    rows = u0.shape[0]
    n_inj = inj_c.shape[0] // 3 - 1
    n_valid = inj_c[3 * n_inj]
    order = [0, 1, 2, 0, 1, 2]
    for k in range(STEPS):
        t = STEPS - 1 - k
        later, now, new = order[k], order[k + 1], order[k + 2]
        step_pass(lams, now, later, new, model)
        add_points(lams, new, inj_c, inj_v, t * n_inj, 0, n_valid)
        wave = t + 1

        def body(i, carry, new=new, wave=wave, first=(k == 0)):
            x0 = pl.multiple_of(i * CX, CX)
            c = waves[wave, pl.ds(x0 + 1, CX)]
            horizontal, vertical = stencil(
                c, waves[wave, pl.ds(x0 + 2, CX)], waves[wave, pl.ds(x0, CX)]
            )
            earlier = lams[new, pl.ds(x0 + 1, CX)]
            if first:
                img_h[pl.ds(x0, CX)] = earlier * horizontal
                img_v[pl.ds(x0, CX)] = earlier * vertical
            else:
                img_h[pl.ds(x0, CX)] = img_h[pl.ds(x0, CX)] + earlier * horizontal
                img_v[pl.ds(x0, CX)] = img_v[pl.ds(x0, CX)] + earlier * vertical
            return carry

        lax.fori_loop(0, rows // CX, body, 0)

    def body(i, carry):
        x0 = pl.multiple_of(i * CX, CX)
        h = img_h[pl.ds(x0, CX)]
        gs_out[pl.ds(x0, CX)] = model[1, pl.ds(x0, CX)] * h + img_v[pl.ds(x0, CX)]
        ga_out[pl.ds(x0, CX)] = 2.0 * model[0, pl.ds(x0, CX)] * h
        return carry

    lax.fori_loop(0, rows // CX, body, 0)


SMEM = pl.BlockSpec(memory_space=pltpu.SMEM)
VMEM = pl.BlockSpec(memory_space=pltpu.VMEM)
PARAMS = pltpu.CompilerParams(vmem_limit_bytes=62 * 1024 * 1024)


def forward_call(src_c, src_v, u0, um1, sp_own, an_own, lo, hi, m_lo, m_hi):
    rows, cross, depth = u0.shape
    wide = cross + 2 * MARGIN
    return pl.pallas_call(
        forward_kernel,
        out_shape=jax.ShapeDtypeStruct((STEPS, rows, cross, depth), jnp.float32),
        in_specs=[SMEM] * 2 + [VMEM] * 8,
        out_specs=VMEM,
        scratch_shapes=[
            pltpu.VMEM((3, rows + 2, wide, depth), jnp.float32),
            pltpu.VMEM((2, rows, wide, depth), jnp.float32),
        ],
        compiler_params=PARAMS,
        cost_estimate=pl.CostEstimate(
            flops=STEPS * 20 * rows * wide * depth,
            bytes_accessed=8 * rows * cross * depth * 4,
            transcendentals=0,
        ),
    )(src_c, src_v, u0, um1, sp_own, an_own, lo, hi, m_lo, m_hi)


def adjoint_call(src_c, src_v, inj_c, inj_v, u0, um1, lam5, lam6, sp_own, an_own, lo, hi, m_lo, m_hi):
    rows, cross, depth = u0.shape
    wide = cross + 2 * MARGIN
    field = jax.ShapeDtypeStruct((rows, wide, depth), jnp.float32)
    return pl.pallas_call(
        adjoint_kernel,
        out_shape=(field, field),
        in_specs=[SMEM] * 4 + [VMEM] * 10,
        out_specs=(VMEM, VMEM),
        scratch_shapes=[
            pltpu.VMEM((STEPS + 1, rows + 2, wide, depth), jnp.float32),
            pltpu.VMEM((3, rows + 2, wide, depth), jnp.float32),
            pltpu.VMEM((rows, wide, depth), jnp.float32),
            pltpu.VMEM((rows, wide, depth), jnp.float32),
            pltpu.VMEM((2, rows, wide, depth), jnp.float32),
        ],
        compiler_params=PARAMS,
        cost_estimate=pl.CostEstimate(
            flops=STEPS * 70 * rows * wide * depth,
            bytes_accessed=10 * rows * cross * depth * 4,
            transcendentals=0,
        ),
    )(src_c, src_v, inj_c, inj_v, u0, um1, lam5, lam6, sp_own, an_own, lo, hi, m_lo, m_hi)


def shards(
    speed_blocks,
    aniso_blocks,
    block_owner,
    block_slot,
    state_now,
    state_prev,
    adjoint_now,
    adjoint_prev,
    source_cell,
    wavelet,
    receiver_cell,
    observed,
):
    count = lax.axis_size("shot")
    me = lax.axis_index("shot")
    capacity = 2 * NEED // count
    slots_all = count * capacity
    rows, cross, depth = state_now.shape
    row_len = cross * depth
    owned = speed_blocks.shape[0]
    nrec = receiver_cell.shape[1]

    wide_y = cross + 2 * MARGIN
    info = jnp.concatenate(
        [
            source_cell.astype(jnp.float32),
            wavelet[0],
            receiver_cell[0].astype(jnp.float32),
        ]
    )
    info = jnp.pad(info, (0, rows * depth - info.shape[0])).reshape(rows, 1, depth)
    fields = (state_now, state_prev, adjoint_now, adjoint_prev)
    top = jnp.concatenate([f[:, cross - HALO :] for f in fields] + [info], axis=1)
    bottom = jnp.concatenate([f[:, :HALO] for f in fields] + [info], axis=1)
    from_below, from_above = exchange(top, bottom, count)

    owners = block_owner[:, 0]
    column_ids = jnp.arange(count, dtype=jnp.int32)
    onehot = (owners[:, None] == column_ids[None, :]).astype(jnp.int32)
    before_count = jnp.sum((jnp.cumsum(onehot, axis=0) - onehot) * onehot, axis=1)
    placed = owners * capacity + before_count
    requests = jnp.full((slots_all,), -1, jnp.int32).at[placed].set(block_slot)
    wanted = lax.all_to_all(
        requests.reshape(count, capacity), "shot", split_axis=0, concat_axis=0, tiled=True
    ).reshape(-1)

    owned_rows = jnp.concatenate([speed_blocks, aniso_blocks], axis=1)
    pick = (wanted[:, None] == jnp.arange(owned, dtype=jnp.int32)[None, :]).astype(jnp.float32)
    outgoing = jnp.dot(pick, owned_rows, precision=HIGH)
    incoming = lax.all_to_all(
        outgoing.reshape(count, capacity, 2 * row_len),
        "shot",
        split_axis=0,
        concat_axis=0,
        tiled=True,
    ).reshape(slots_all, 2 * row_len)
    place_hot = (placed[:, None] == jnp.arange(slots_all, dtype=jnp.int32)[None, :]).astype(
        jnp.float32
    )
    fetched = jnp.dot(place_hot, incoming, precision=HIGH)
    speed_own = fetched[:, :row_len].reshape(rows, cross, depth)
    aniso_own = fetched[:, row_len:].reshape(rows, cross, depth)

    model_below, model_above = exchange(
        jnp.concatenate([speed_own[:, cross - HALO :], aniso_own[:, cross - HALO :]], axis=1),
        jnp.concatenate([speed_own[:, :HALO], aniso_own[:, :HALO]], axis=1),
        count,
    )
    info_below = from_below[:, 4 * HALO].reshape(-1)
    info_above = from_above[:, 4 * HALO].reshape(-1)

    def unpack(flat):
        src = flat[0].astype(jnp.int32)
        wav = flat[1 : 1 + STEPS]
        rec = flat[1 + STEPS : 1 + STEPS + nrec].astype(jnp.int32)
        return src, wav, rec

    src_below, wav_below, rec_below = unpack(info_below)
    src_above, wav_above, rec_above = unpack(info_above)

    lower_offset = MARGIN - cross
    upper_offset = MARGIN + cross
    sx, sy, sz = [
        jnp.stack(parts)
        for parts in zip(
            cell_coords(source_cell[0], cross, MARGIN),
            cell_coords(src_below, cross, lower_offset),
            cell_coords(src_above, cross, upper_offset),
        )
    ]
    wav_all = jnp.stack([wavelet[0], wav_below, wav_above], axis=1)
    rx_own, ry_own, rz_own = cell_coords(receiver_cell[0], cross, MARGIN)
    rx, ry, rz = [
        jnp.concatenate(parts)
        for parts in zip(
            (rx_own, ry_own, rz_own),
            cell_coords(rec_below, cross, lower_offset),
            cell_coords(rec_above, cross, upper_offset),
        )
    ]

    valid_src = (sy >= 0) & (sy < wide_y)
    src_coords = jnp.stack([sx, jnp.where(valid_src, sy, 0), sz], axis=1).reshape(-1)
    src_vals = jnp.where(valid_src[None, :], wav_all, 0.0).reshape(-1)
    halos = (from_below, from_above, model_below, model_above)
    waves_own = forward_call(src_coords, src_vals, state_now, state_prev, speed_own, aniso_own, *halos)
    final_wave = waves_own[STEPS - 1]
    flat_cells = (
        jnp.arange(STEPS, dtype=jnp.int32)[:, None] * (rows * row_len) + receiver_cell[0][None, :]
    )
    synthetic = waves_own.reshape(-1)[flat_cells]
    misfit_own = synthetic - observed[0]
    mis_below, mis_above = exchange(misfit_own, misfit_own, count)
    valid_rec = (ry >= MARGIN - HALO + 1) & (ry < MARGIN + cross + HALO - 1)
    valid_rec = valid_rec.at[:nrec].set(True)
    total = 3 * nrec
    dest = jnp.where(valid_rec, jnp.cumsum(valid_rec.astype(jnp.int32)) - 1, total)
    coords = jnp.stack([rx, ry, rz], axis=1)
    inj_coords = jnp.zeros((total + 1, 3), jnp.int32).at[dest].set(coords, mode="drop")
    inj_coords = inj_coords.at[total, 0].set(jnp.sum(valid_rec.astype(jnp.int32)))
    inj_coords = inj_coords.reshape(-1)
    injected = jnp.concatenate([misfit_own, mis_below, mis_above], axis=1)
    inj_vals = jnp.zeros((STEPS, total), jnp.float32).at[:, dest].set(injected, mode="drop").reshape(-1)
    gradient_speed, gradient_aniso = adjoint_call(
        src_coords, src_vals, inj_coords, inj_vals, state_now, state_prev, adjoint_now, adjoint_prev,
        speed_own, aniso_own, *halos
    )
    speeds = jnp.concatenate(
        [model_below[:, HALO - 1 : HALO], speed_own, model_above[:, 0:1]], axis=1
    )

    position = (me + SPLIT // 2) % SPLIT
    has_below = jnp.logical_and(position > 0, me > 0).astype(jnp.float32)
    has_above = jnp.logical_and(position < SPLIT - 1, me < count - 1).astype(jnp.float32)
    wide = speeds.shape[1]
    layer = lax.broadcasted_iota(jnp.int32, (1, wide, 1), 1)
    exists = jnp.where(layer < 1, has_below, jnp.where(layer >= 1 + cross, has_above, 1.0))
    exists = jnp.broadcast_to(exists, speeds.shape)

    lo, hi = 1, 1 + cross
    grads = jnp.stack([gradient_speed, gradient_aniso])[:, :, MARGIN - 1 : MARGIN + cross + 1]
    center_g = grads[:, :, lo:hi]
    center_s = speeds[:, lo:hi]

    def neighbour(v, axis, step):
        nd = v.ndim
        ax = nd - 3 + axis
        if axis == 1:
            return lax.slice_in_dim(v, lo + step, hi + step, axis=ax)
        center = lax.slice_in_dim(v, lo, hi, axis=nd - 2)
        pad = [(0, 0)] * nd
        pad[ax] = (1, 1)
        padded = jnp.pad(center, pad)
        length = center.shape[ax]
        return lax.slice_in_dim(padded, 1 + step, 1 + step + length, axis=ax)

    totals = jnp.zeros_like(center_g)
    for axis in (0, 1, 2):
        for step in (1, -1):
            g_n = neighbour(grads, axis, step)
            s_n = neighbour(speeds, axis, step)
            e_n = neighbour(exists, axis, step)
            contrast = (s_n - center_s) / EDGE_SCALE
            weight = e_n / (1.0 + contrast * contrast)
            totals = totals + weight[None] * (g_n - center_g)
    smoothed = center_g + KAPPA_RATE * totals

    rows_out = jnp.transpose(smoothed, (1, 0, 2, 3)).reshape(rows, 2 * row_len)
    returning = jnp.dot(place_hot.T, rows_out, precision=HIGH)
    returned = lax.all_to_all(
        returning.reshape(count, capacity, 2 * row_len),
        "shot",
        split_axis=0,
        concat_axis=0,
        tiled=True,
    ).reshape(slots_all, 2 * row_len)
    summed = jnp.dot(pick.T, returned, precision=HIGH)
    return (final_wave, (summed * IMAGE_GAIN).reshape(owned, 2, row_len))


def solution(mesh):
    placed = (
        P(("groups", "shot"), None),
        P(("groups", "shot"), None),
        P(("groups", "shot"), None),
        P(("groups", "shot")),
        P(("groups", "shot"), None, None),
        P(("groups", "shot"), None, None),
        P(("groups", "shot"), None, None),
        P(("groups", "shot"), None, None),
        P(("groups", "shot")),
        P(("groups", "shot"), None),
        P(("groups", "shot"), None),
        P(("groups", "shot"), None, None),
    )
    return jax.shard_map(
        shards,
        mesh=mesh,
        in_specs=placed,
        out_specs=(P(("groups", "shot"), None, None), P(("groups", "shot"), None, None)),
        check_vma=False,
    )
```

```python
import jax
import jax.numpy as jnp
from jax import lax
from jax.sharding import PartitionSpec as P

NEED = 128
STEPS = 4
SPLIT = 8


EDGE_SCALE = 0.02
KAPPA_RATE = 0.15
IMAGE_GAIN = 0.03125


def extended(array, sides, width):
    for axis, dim in sides:
        count, length = (lax.axis_size(axis), array.shape[dim])
        up = [(i, i + 1) for i in range(count - 1) if (i + SPLIT // 2) % SPLIT < SPLIT - 1]
        down = [(j, i) for i, j in up]
        last = lax.slice_in_dim(array, length - width, length, axis=dim)
        leading = lax.slice_in_dim(array, 0, width, axis=dim)
        before = lax.ppermute(last, axis, up)
        after = lax.ppermute(leading, axis, down)
        array = jnp.concatenate([before, array, after], axis=dim)
    return array


def cross_mask(widened, axis_at):
    position = (lax.axis_index("shot") + SPLIT // 2) % SPLIT
    extent = widened.shape[axis_at]
    row_index = lax.broadcasted_iota(jnp.int32, (extent,), 0)
    keep_lower = jnp.logical_or(row_index > 0, position > 0)
    keep_upper = jnp.logical_or(row_index < extent - 1, position < SPLIT - 1)
    keep_mask = jnp.logical_and(keep_lower, keep_upper).astype(widened.dtype)
    dims_out = [1] * widened.ndim
    dims_out[axis_at] = extent
    return widened * keep_mask.reshape(dims_out)


def forward_rims(wavefield):
    return cross_mask(extended(wavefield, (("shot", 1),), 1), 1)


def adjoint_rims_of(wavefield):
    return cross_mask(extended(wavefield, (("shot", 1),), 1), 1)


def image_rims_of(stacked):
    return cross_mask(extended(stacked, (("shot", 2),), 1), 2)


def curvatures(widened):
    center = widened[..., 1:-1, :]
    along_cross = widened[..., 2:, :] + widened[..., :-2, :]
    inline_pad = [(0, 0)] * (center.ndim - 3) + [(1, 1), (0, 0), (0, 0)]
    padded_inline = jnp.pad(center, inline_pad)
    along_inline = padded_inline[..., 2:, :, :] + padded_inline[..., :-2, :, :]
    depth_pad = [(0, 0)] * (center.ndim - 1) + [(1, 1)]
    padded_depth = jnp.pad(center, depth_pad)
    along_depth = padded_depth[..., 2:] + padded_depth[..., :-2]
    horizontal = along_inline + along_cross - 4.0 * center
    vertical = along_depth - 2.0 * center
    return (horizontal, vertical)


def diffuse(widened):
    center = widened[..., 1:-1, :]
    inline_pad = [(0, 0)] * (center.ndim - 4) + [(1, 1), (0, 0), (0, 0), (0, 0)]
    padded_inline = jnp.pad(center, inline_pad)
    depth_pad = [(0, 0)] * (center.ndim - 1) + [(1, 1)]
    padded_depth = jnp.pad(center, depth_pad)
    beside_all = [
        padded_inline[..., 2:, :, :, :],
        padded_inline[..., :-2, :, :, :],
        widened[..., 2:, :],
        widened[..., :-2, :],
        padded_depth[..., 2:],
        padded_depth[..., :-2],
    ]
    images = center[..., 0:2, :, :]
    speed_here = center[..., 2:3, :, :]
    totals = jnp.zeros_like(images)
    for beside in beside_all:
        contrast = (beside[..., 2:3, :, :] - speed_here) / EDGE_SCALE
        weight = beside[..., 3:4, :, :] / (1.0 + contrast * contrast)
        totals = totals + weight * (beside[..., 0:2, :, :] - images)
    return images + KAPPA_RATE * totals


def shards(
    speed_blocks,
    aniso_blocks,
    block_owner,
    block_slot,
    state_now,
    state_prev,
    adjoint_now,
    adjoint_prev,
    source_cell,
    wavelet,
    receiver_cell,
    observed,
):
    shot_count = lax.axis_size("shot")
    capacity = 2 * NEED // shot_count
    slots_all = shot_count * capacity
    owners = block_owner[:, 0]
    column_ids = jnp.arange(shot_count, dtype=jnp.int32)
    onehot = (owners[:, None] == column_ids[None, :]).astype(jnp.int32)
    before_count = jnp.sum((jnp.cumsum(onehot, axis=0) - onehot) * onehot, axis=1)
    placed = owners * capacity + before_count
    requests = jnp.full((slots_all,), -1, jnp.int32).at[placed].set(block_slot)
    wanted = lax.all_to_all(
        requests.reshape(shot_count, capacity), "shot", split_axis=0, concat_axis=0, tiled=True
    )
    row_len = speed_blocks.shape[1]
    owned = speed_blocks.shape[0]
    wanted = wanted.reshape(-1)
    owned_rows = jnp.concatenate([speed_blocks, aniso_blocks], axis=1)
    pick = (wanted[:, None] == jnp.arange(owned, dtype=jnp.int32)[None, :]).astype(jnp.float32)
    outgoing = jnp.dot(pick, owned_rows, precision=lax.Precision.HIGHEST)
    incoming = lax.all_to_all(
        outgoing.reshape(shot_count, capacity, 2 * row_len),
        "shot",
        split_axis=0,
        concat_axis=0,
        tiled=True,
    ).reshape(slots_all, 2 * row_len)
    place_hot = (placed[:, None] == jnp.arange(slots_all, dtype=jnp.int32)[None, :]).astype(
        jnp.float32
    )
    fetched = jnp.dot(place_hot, incoming, precision=lax.Precision.HIGHEST)
    grid_dims = state_now.shape
    speeds = fetched[:, :row_len].reshape(grid_dims)
    hfactor = 1.0 + 2.0 * fetched[:, row_len:].reshape(grid_dims)
    previous = state_prev
    current = state_now
    rows_all = grid_dims[0] * grid_dims[1]
    depth = grid_dims[2]
    row_hot = (
        receiver_cell[0][:, None] // depth == jnp.arange(rows_all, dtype=jnp.int32)[None, :]
    ).astype(jnp.float32)
    lane_hot = receiver_cell[0][:, None] % depth == jnp.arange(depth, dtype=jnp.int32)[None, :]
    saved_first = []
    saved_second = []
    misfits = []
    for time_step in range(STEPS):
        horizontal, vertical = curvatures(forward_rims(current))
        advanced = 2.0 * current - previous + speeds * (hfactor * horizontal + vertical)
        advanced = (
            advanced.reshape(-1).at[source_cell[0]].add(wavelet[0, time_step]).reshape(grid_dims)
        )
        picked = jnp.dot(
            row_hot, advanced.reshape(rows_all, depth), precision=lax.Precision.HIGHEST
        )
        synthetic = jnp.sum(jnp.where(lane_hot, picked, 0.0), axis=1)
        misfits.append(synthetic - observed[0, time_step])
        saved_first.append(horizontal)
        saved_second.append(vertical)
        previous, current = (current, advanced)
    later_adjoint = adjoint_prev
    adjoint = adjoint_now
    image_horizontal = jnp.zeros(grid_dims, jnp.float32)
    image_vertical = jnp.zeros(grid_dims, jnp.float32)
    for time_step in range(STEPS - 1, -1, -1):
        horizontal, vertical = curvatures(adjoint_rims_of(adjoint))
        wave_horizontal = saved_first[time_step]
        wave_vertical = saved_second[time_step]
        earlier = 2.0 * adjoint - later_adjoint + speeds * (hfactor * horizontal + vertical)
        spread = jnp.where(lane_hot, misfits[time_step][:, None], 0.0)
        injected = jnp.dot(row_hot.T, spread, precision=lax.Precision.HIGHEST)
        earlier = earlier + injected.reshape(grid_dims)
        image_horizontal = image_horizontal + earlier * wave_horizontal
        image_vertical = image_vertical + earlier * wave_vertical
        later_adjoint, adjoint = (adjoint, earlier)
    gradient_speed = hfactor * image_horizontal + image_vertical
    gradient_aniso = 2.0 * speeds * image_horizontal
    stacked = jnp.stack([gradient_speed, gradient_aniso, speeds, jnp.ones_like(speeds)], axis=1)
    smoothed = diffuse(image_rims_of(stacked))
    rows_out = smoothed.reshape(NEED, 2 * row_len)
    returning = jnp.dot(place_hot.T, rows_out, precision=lax.Precision.HIGHEST)
    returned = lax.all_to_all(
        returning.reshape(shot_count, capacity, 2 * row_len),
        "shot",
        split_axis=0,
        concat_axis=0,
        tiled=True,
    ).reshape(slots_all, 2 * row_len)
    summed = jnp.dot(pick.T, returned, precision=lax.Precision.HIGHEST)
    return (current, (summed * IMAGE_GAIN).reshape(owned, 2, row_len))


def solution(mesh):
    placed = (
        P(("groups", "shot"), None),
        P(("groups", "shot"), None),
        P(("groups", "shot"), None),
        P(("groups", "shot")),
        P(("groups", "shot"), None, None),
        P(("groups", "shot"), None, None),
        P(("groups", "shot"), None, None),
        P(("groups", "shot"), None, None),
        P(("groups", "shot")),
        P(("groups", "shot"), None),
        P(("groups", "shot"), None),
        P(("groups", "shot"), None, None),
    )
    return jax.shard_map(
        shards,
        mesh=mesh,
        in_specs=placed,
        out_specs=(P(("groups", "shot"), None, None), P(("groups", "shot"), None, None)),
        check_vma=False,
    )
```

```python
import jax
import jax.numpy as jnp
from jax import lax
from jax.sharding import PartitionSpec as P

NEED = 128
STEPS = 4
SPLIT = 8


EDGE_SCALE = 0.02
KAPPA_RATE = 0.15
IMAGE_GAIN = 0.03125


def extended(array, sides, width):
    for axis, dim in sides:
        count, length = (lax.axis_size(axis), array.shape[dim])
        up = [(i, i + 1) for i in range(count - 1) if (i + SPLIT // 2) % SPLIT < SPLIT - 1]
        down = [(j, i) for i, j in up]
        last = lax.slice_in_dim(array, length - width, length, axis=dim)
        leading = lax.slice_in_dim(array, 0, width, axis=dim)
        before = lax.ppermute(last, axis, up)
        after = lax.ppermute(leading, axis, down)
        array = jnp.concatenate([before, array, after], axis=dim)
    return array


def cross_mask(widened, axis_at):
    position = (lax.axis_index("shot") + SPLIT // 2) % SPLIT
    extent = widened.shape[axis_at]
    row_index = lax.broadcasted_iota(jnp.int32, (extent,), 0)
    keep_lower = jnp.logical_or(row_index > 0, position > 0)
    keep_upper = jnp.logical_or(row_index < extent - 1, position < SPLIT - 1)
    keep_mask = jnp.logical_and(keep_lower, keep_upper).astype(widened.dtype)
    dims_out = [1] * widened.ndim
    dims_out[axis_at] = extent
    return widened * keep_mask.reshape(dims_out)


def forward_rims(wavefield):
    return cross_mask(extended(wavefield, (("shot", 1),), 1), 1)


def adjoint_rims_of(wavefield):
    return cross_mask(extended(wavefield, (("shot", 1),), 1), 1)


def image_rims_of(stacked):
    return cross_mask(extended(stacked, (("shot", 2),), 1), 2)


def curvatures(widened):
    center = widened[..., 1:-1, :]
    along_cross = widened[..., 2:, :] + widened[..., :-2, :]
    inline_pad = [(0, 0)] * (center.ndim - 3) + [(1, 1), (0, 0), (0, 0)]
    padded_inline = jnp.pad(center, inline_pad)
    along_inline = padded_inline[..., 2:, :, :] + padded_inline[..., :-2, :, :]
    depth_pad = [(0, 0)] * (center.ndim - 1) + [(1, 1)]
    padded_depth = jnp.pad(center, depth_pad)
    along_depth = padded_depth[..., 2:] + padded_depth[..., :-2]
    horizontal = along_inline + along_cross - 4.0 * center
    vertical = along_depth - 2.0 * center
    return (horizontal, vertical)


def diffuse(widened):
    center = widened[..., 1:-1, :]
    inline_pad = [(0, 0)] * (center.ndim - 4) + [(1, 1), (0, 0), (0, 0), (0, 0)]
    padded_inline = jnp.pad(center, inline_pad)
    depth_pad = [(0, 0)] * (center.ndim - 1) + [(1, 1)]
    padded_depth = jnp.pad(center, depth_pad)
    beside_all = [
        padded_inline[..., 2:, :, :, :],
        padded_inline[..., :-2, :, :, :],
        widened[..., 2:, :],
        widened[..., :-2, :],
        padded_depth[..., 2:],
        padded_depth[..., :-2],
    ]
    images = center[..., 0:2, :, :]
    speed_here = center[..., 2:3, :, :]
    totals = jnp.zeros_like(images)
    for beside in beside_all:
        contrast = (beside[..., 2:3, :, :] - speed_here) / EDGE_SCALE
        weight = beside[..., 3:4, :, :] / (1.0 + contrast * contrast)
        totals = totals + weight * (beside[..., 0:2, :, :] - images)
    return images + KAPPA_RATE * totals


def shards(
    speed_blocks,
    aniso_blocks,
    block_owner,
    block_slot,
    state_now,
    state_prev,
    adjoint_now,
    adjoint_prev,
    source_cell,
    wavelet,
    receiver_cell,
    observed,
):
    shot_count = lax.axis_size("shot")
    capacity = 2 * NEED // shot_count
    slots_all = shot_count * capacity
    owners = block_owner[:, 0]
    column_ids = jnp.arange(shot_count, dtype=jnp.int32)
    onehot = (owners[:, None] == column_ids[None, :]).astype(jnp.int32)
    before_count = jnp.sum((jnp.cumsum(onehot, axis=0) - onehot) * onehot, axis=1)
    placed = owners * capacity + before_count
    gathered = lax.all_gather(jnp.stack([owners, block_slot]), "shot")
    mine = gathered[:, 0] == lax.axis_index("shot")
    order = jnp.cumsum(mine.astype(jnp.int32), axis=1) - 1
    hit = mine[:, :, None] & (order[:, :, None] == jnp.arange(capacity, dtype=jnp.int32))
    wanted = jnp.where(
        jnp.any(hit, axis=1), jnp.sum(jnp.where(hit, gathered[:, 1][:, :, None], 0), axis=1), -1
    )
    row_len = speed_blocks.shape[1]
    owned = speed_blocks.shape[0]
    wanted = wanted.reshape(-1)
    owned_rows = jnp.concatenate([speed_blocks, aniso_blocks], axis=1)
    pick = (wanted[:, None] == jnp.arange(owned, dtype=jnp.int32)[None, :]).astype(jnp.float32)
    outgoing = jnp.dot(pick, owned_rows, precision=lax.Precision.HIGHEST)
    incoming = lax.all_to_all(
        outgoing.reshape(shot_count, capacity, 2 * row_len),
        "shot",
        split_axis=0,
        concat_axis=0,
        tiled=True,
    ).reshape(slots_all, 2 * row_len)
    place_hot = (placed[:, None] == jnp.arange(slots_all, dtype=jnp.int32)[None, :]).astype(
        jnp.float32
    )
    fetched = jnp.dot(place_hot, incoming, precision=lax.Precision.HIGHEST)
    grid_dims = state_now.shape
    speeds = fetched[:, :row_len].reshape(grid_dims)
    hfactor = 1.0 + 2.0 * fetched[:, row_len:].reshape(grid_dims)
    previous = state_prev
    current = state_now
    rows_all = grid_dims[0] * grid_dims[1]
    depth = grid_dims[2]
    row_hot = (
        receiver_cell[0][:, None] // depth == jnp.arange(rows_all, dtype=jnp.int32)[None, :]
    ).astype(jnp.float32)
    lane_hot = receiver_cell[0][:, None] % depth == jnp.arange(depth, dtype=jnp.int32)[None, :]
    saved_first = []
    saved_second = []
    misfits = []
    for time_step in range(STEPS):
        horizontal, vertical = curvatures(forward_rims(current))
        advanced = 2.0 * current - previous + speeds * (hfactor * horizontal + vertical)
        advanced = (
            advanced.reshape(-1).at[source_cell[0]].add(wavelet[0, time_step]).reshape(grid_dims)
        )
        picked = jnp.dot(
            row_hot, advanced.reshape(rows_all, depth), precision=lax.Precision.HIGHEST
        )
        synthetic = jnp.sum(jnp.where(lane_hot, picked, 0.0), axis=1)
        misfits.append(synthetic - observed[0, time_step])
        saved_first.append(horizontal)
        saved_second.append(vertical)
        previous, current = (current, advanced)
    later_adjoint = adjoint_prev
    adjoint = adjoint_now
    image_horizontal = jnp.zeros(grid_dims, jnp.float32)
    image_vertical = jnp.zeros(grid_dims, jnp.float32)
    for time_step in range(STEPS - 1, -1, -1):
        horizontal, vertical = curvatures(adjoint_rims_of(adjoint))
        wave_horizontal = saved_first[time_step]
        wave_vertical = saved_second[time_step]
        earlier = 2.0 * adjoint - later_adjoint + speeds * (hfactor * horizontal + vertical)
        spread = jnp.where(lane_hot, misfits[time_step][:, None], 0.0)
        injected = jnp.dot(row_hot.T, spread, precision=lax.Precision.HIGHEST)
        earlier = earlier + injected.reshape(grid_dims)
        image_horizontal = image_horizontal + earlier * wave_horizontal
        image_vertical = image_vertical + earlier * wave_vertical
        later_adjoint, adjoint = (adjoint, earlier)
    gradient_speed = hfactor * image_horizontal + image_vertical
    gradient_aniso = 2.0 * speeds * image_horizontal
    stacked = jnp.stack([gradient_speed, gradient_aniso, speeds, jnp.ones_like(speeds)], axis=1)
    smoothed = diffuse(image_rims_of(stacked))
    rows_out = smoothed.reshape(NEED, 2 * row_len)
    returning = jnp.dot(place_hot.T, rows_out, precision=lax.Precision.HIGHEST)
    returned = lax.all_to_all(
        returning.reshape(shot_count, capacity, 2 * row_len),
        "shot",
        split_axis=0,
        concat_axis=0,
        tiled=True,
    ).reshape(slots_all, 2 * row_len)
    summed = jnp.dot(pick.T, returned, precision=lax.Precision.HIGHEST)
    return (current, (summed * IMAGE_GAIN).reshape(owned, 2, row_len))


def solution(mesh):
    placed = (
        P(("groups", "shot"), None),
        P(("groups", "shot"), None),
        P(("groups", "shot"), None),
        P(("groups", "shot")),
        P(("groups", "shot"), None, None),
        P(("groups", "shot"), None, None),
        P(("groups", "shot"), None, None),
        P(("groups", "shot"), None, None),
        P(("groups", "shot")),
        P(("groups", "shot"), None),
        P(("groups", "shot"), None),
        P(("groups", "shot"), None, None),
    )
    return jax.shard_map(
        shards,
        mesh=mesh,
        in_specs=placed,
        out_specs=(P(("groups", "shot"), None, None), P(("groups", "shot"), None, None)),
        check_vma=False,
    )
```

```python
import jax
import jax.numpy as jnp
from jax import lax
from jax.sharding import PartitionSpec as P

NEED = 128
STEPS = 4
SPLIT = 8


EDGE_SCALE = 0.02
KAPPA_RATE = 0.15
IMAGE_GAIN = 0.03125


def extended(array, sides, width):
    for axis, dim in sides:
        count, length = (lax.axis_size(axis), array.shape[dim])
        joined = [i for i in range(count - 1) if (i + SPLIT // 2) % SPLIT < SPLIT - 1]
        inner = [(i, i + 1) for i in joined if i % 2 == 0]
        outer = [(i, i + 1) for i in joined if i % 2 == 1]
        inner = inner + [(j, i) for i, j in inner]
        outer = outer + [(j, i) for i, j in outer]
        last = lax.slice_in_dim(array, length - width, length, axis=dim)
        leading = lax.slice_in_dim(array, 0, width, axis=dim)
        even = lax.axis_index(axis) % 2 == 0
        got_inner = lax.ppermute(jnp.where(even, last, leading), axis, inner)
        got_outer = lax.ppermute(jnp.where(even, leading, last), axis, outer)
        before = jnp.where(even, got_outer, got_inner)
        after = jnp.where(even, got_inner, got_outer)
        array = jnp.concatenate([before, array, after], axis=dim)
    return array


def cross_mask(widened, axis_at):
    position = (lax.axis_index("shot") + SPLIT // 2) % SPLIT
    extent = widened.shape[axis_at]
    row_index = lax.broadcasted_iota(jnp.int32, (extent,), 0)
    keep_lower = jnp.logical_or(row_index > 0, position > 0)
    keep_upper = jnp.logical_or(row_index < extent - 1, position < SPLIT - 1)
    keep_mask = jnp.logical_and(keep_lower, keep_upper).astype(widened.dtype)
    dims_out = [1] * widened.ndim
    dims_out[axis_at] = extent
    return widened * keep_mask.reshape(dims_out)


def forward_rims(wavefield):
    return cross_mask(extended(wavefield, (("shot", 1),), 1), 1)


def adjoint_rims_of(wavefield):
    return cross_mask(extended(wavefield, (("shot", 1),), 1), 1)


def image_rims_of(stacked):
    return cross_mask(extended(stacked, (("shot", 2),), 1), 2)


def curvatures(widened):
    center = widened[..., 1:-1, :]
    along_cross = widened[..., 2:, :] + widened[..., :-2, :]
    inline_pad = [(0, 0)] * (center.ndim - 3) + [(1, 1), (0, 0), (0, 0)]
    padded_inline = jnp.pad(center, inline_pad)
    along_inline = padded_inline[..., 2:, :, :] + padded_inline[..., :-2, :, :]
    depth_pad = [(0, 0)] * (center.ndim - 1) + [(1, 1)]
    padded_depth = jnp.pad(center, depth_pad)
    along_depth = padded_depth[..., 2:] + padded_depth[..., :-2]
    horizontal = along_inline + along_cross - 4.0 * center
    vertical = along_depth - 2.0 * center
    return (horizontal, vertical)


def diffuse(widened):
    center = widened[..., 1:-1, :]
    inline_pad = [(0, 0)] * (center.ndim - 4) + [(1, 1), (0, 0), (0, 0), (0, 0)]
    padded_inline = jnp.pad(center, inline_pad)
    depth_pad = [(0, 0)] * (center.ndim - 1) + [(1, 1)]
    padded_depth = jnp.pad(center, depth_pad)
    beside_all = [
        padded_inline[..., 2:, :, :, :],
        padded_inline[..., :-2, :, :, :],
        widened[..., 2:, :],
        widened[..., :-2, :],
        padded_depth[..., 2:],
        padded_depth[..., :-2],
    ]
    images = center[..., 0:2, :, :]
    speed_here = center[..., 2:3, :, :]
    totals = jnp.zeros_like(images)
    for beside in beside_all:
        contrast = (beside[..., 2:3, :, :] - speed_here) / EDGE_SCALE
        weight = beside[..., 3:4, :, :] / (1.0 + contrast * contrast)
        totals = totals + weight * (beside[..., 0:2, :, :] - images)
    return images + KAPPA_RATE * totals


def shards(
    speed_blocks,
    aniso_blocks,
    block_owner,
    block_slot,
    state_now,
    state_prev,
    adjoint_now,
    adjoint_prev,
    source_cell,
    wavelet,
    receiver_cell,
    observed,
):
    shot_count = lax.axis_size("shot")
    capacity = 2 * NEED // shot_count
    slots_all = shot_count * capacity
    owners = block_owner[:, 0]
    column_ids = jnp.arange(shot_count, dtype=jnp.int32)
    onehot = (owners[:, None] == column_ids[None, :]).astype(jnp.int32)
    before_count = jnp.sum((jnp.cumsum(onehot, axis=0) - onehot) * onehot, axis=1)
    placed = owners * capacity + before_count
    requests = jnp.full((slots_all,), -1, jnp.int32).at[placed].set(block_slot)
    wanted = lax.all_to_all(
        requests.reshape(shot_count, capacity), "shot", split_axis=0, concat_axis=0, tiled=True
    )
    row_len = speed_blocks.shape[1]
    owned = speed_blocks.shape[0]
    wanted = wanted.reshape(-1)
    owned_rows = jnp.concatenate([speed_blocks, aniso_blocks], axis=1)
    pick = (wanted[:, None] == jnp.arange(owned, dtype=jnp.int32)[None, :]).astype(jnp.float32)
    outgoing = jnp.dot(pick, owned_rows, precision=lax.Precision.HIGHEST)
    incoming = lax.all_to_all(
        outgoing.reshape(shot_count, capacity, 2 * row_len),
        "shot",
        split_axis=0,
        concat_axis=0,
        tiled=True,
    ).reshape(slots_all, 2 * row_len)
    place_hot = (placed[:, None] == jnp.arange(slots_all, dtype=jnp.int32)[None, :]).astype(
        jnp.float32
    )
    fetched = jnp.dot(place_hot, incoming, precision=lax.Precision.HIGHEST)
    grid_dims = state_now.shape
    speeds = fetched[:, :row_len].reshape(grid_dims)
    hfactor = 1.0 + 2.0 * fetched[:, row_len:].reshape(grid_dims)
    previous = state_prev
    current = state_now
    rows_all = grid_dims[0] * grid_dims[1]
    depth = grid_dims[2]
    row_hot = (
        receiver_cell[0][:, None] // depth == jnp.arange(rows_all, dtype=jnp.int32)[None, :]
    ).astype(jnp.float32)
    lane_hot = receiver_cell[0][:, None] % depth == jnp.arange(depth, dtype=jnp.int32)[None, :]
    saved_first = []
    saved_second = []
    misfits = []
    for time_step in range(STEPS):
        horizontal, vertical = curvatures(forward_rims(current))
        advanced = 2.0 * current - previous + speeds * (hfactor * horizontal + vertical)
        advanced = (
            advanced.reshape(-1).at[source_cell[0]].add(wavelet[0, time_step]).reshape(grid_dims)
        )
        picked = jnp.dot(
            row_hot, advanced.reshape(rows_all, depth), precision=lax.Precision.HIGHEST
        )
        synthetic = jnp.sum(jnp.where(lane_hot, picked, 0.0), axis=1)
        misfits.append(synthetic - observed[0, time_step])
        saved_first.append(horizontal)
        saved_second.append(vertical)
        previous, current = (current, advanced)
    later_adjoint = adjoint_prev
    adjoint = adjoint_now
    image_horizontal = jnp.zeros(grid_dims, jnp.float32)
    image_vertical = jnp.zeros(grid_dims, jnp.float32)
    for time_step in range(STEPS - 1, -1, -1):
        horizontal, vertical = curvatures(adjoint_rims_of(adjoint))
        wave_horizontal = saved_first[time_step]
        wave_vertical = saved_second[time_step]
        earlier = 2.0 * adjoint - later_adjoint + speeds * (hfactor * horizontal + vertical)
        spread = jnp.where(lane_hot, misfits[time_step][:, None], 0.0)
        injected = jnp.dot(row_hot.T, spread, precision=lax.Precision.HIGHEST)
        earlier = earlier + injected.reshape(grid_dims)
        image_horizontal = image_horizontal + earlier * wave_horizontal
        image_vertical = image_vertical + earlier * wave_vertical
        later_adjoint, adjoint = (adjoint, earlier)
    gradient_speed = hfactor * image_horizontal + image_vertical
    gradient_aniso = 2.0 * speeds * image_horizontal
    stacked = jnp.stack([gradient_speed, gradient_aniso, speeds, jnp.ones_like(speeds)], axis=1)
    smoothed = diffuse(image_rims_of(stacked))
    rows_out = smoothed.reshape(NEED, 2 * row_len)
    returning = jnp.dot(place_hot.T, rows_out, precision=lax.Precision.HIGHEST)
    returned = lax.all_to_all(
        returning.reshape(shot_count, capacity, 2 * row_len),
        "shot",
        split_axis=0,
        concat_axis=0,
        tiled=True,
    ).reshape(slots_all, 2 * row_len)
    summed = jnp.dot(pick.T, returned, precision=lax.Precision.HIGHEST)
    return (current, (summed * IMAGE_GAIN).reshape(owned, 2, row_len))


def solution(mesh):
    placed = (
        P(("groups", "shot"), None),
        P(("groups", "shot"), None),
        P(("groups", "shot"), None),
        P(("groups", "shot")),
        P(("groups", "shot"), None, None),
        P(("groups", "shot"), None, None),
        P(("groups", "shot"), None, None),
        P(("groups", "shot"), None, None),
        P(("groups", "shot")),
        P(("groups", "shot"), None),
        P(("groups", "shot"), None),
        P(("groups", "shot"), None, None),
    )
    return jax.shard_map(
        shards,
        mesh=mesh,
        in_specs=placed,
        out_specs=(P(("groups", "shot"), None, None), P(("groups", "shot"), None, None)),
        check_vma=False,
    )
```

```python
import jax
import jax.numpy as jnp
from jax import lax
from jax.sharding import PartitionSpec as P

NEED = 128
STEPS = 4
SPLIT = 8


EDGE_SCALE = 0.02
KAPPA_RATE = 0.15
IMAGE_GAIN = 0.03125


def extended(array, sides, width):
    for axis, dim in sides:
        count, length = (lax.axis_size(axis), array.shape[dim])
        joined = [i for i in range(count - 1) if (i + SPLIT // 2) % SPLIT < SPLIT - 1]
        inner = [(i, i + 1) for i in joined if i % 2 == 0]
        outer = [(i, i + 1) for i in joined if i % 2 == 1]
        inner = inner + [(j, i) for i, j in inner]
        outer = outer + [(j, i) for i, j in outer]
        last = lax.slice_in_dim(array, length - width, length, axis=dim)
        leading = lax.slice_in_dim(array, 0, width, axis=dim)
        even = lax.axis_index(axis) % 2 == 0
        got_inner = lax.ppermute(jnp.where(even, last, leading), axis, inner)
        got_outer = lax.ppermute(jnp.where(even, leading, last), axis, outer)
        before = jnp.where(even, got_outer, got_inner)
        after = jnp.where(even, got_inner, got_outer)
        array = jnp.concatenate([before, array, after], axis=dim)
    return array


def cross_mask(widened, axis_at):
    position = (lax.axis_index("shot") + SPLIT // 2) % SPLIT
    extent = widened.shape[axis_at]
    row_index = lax.broadcasted_iota(jnp.int32, (extent,), 0)
    keep_lower = jnp.logical_or(row_index > 0, position > 0)
    keep_upper = jnp.logical_or(row_index < extent - 1, position < SPLIT - 1)
    keep_mask = jnp.logical_and(keep_lower, keep_upper).astype(widened.dtype)
    dims_out = [1] * widened.ndim
    dims_out[axis_at] = extent
    return widened * keep_mask.reshape(dims_out)


def forward_rims(wavefield):
    return cross_mask(extended(wavefield, (("shot", 1),), 1), 1)


def adjoint_rims_of(wavefield):
    return cross_mask(extended(wavefield, (("shot", 1),), 1), 1)


def image_rims_of(stacked):
    return cross_mask(extended(stacked, (("shot", 2),), 1), 2)


def curvatures(widened):
    center = widened[..., 1:-1, :]
    along_cross = widened[..., 2:, :] + widened[..., :-2, :]
    inline_pad = [(0, 0)] * (center.ndim - 3) + [(1, 1), (0, 0), (0, 0)]
    padded_inline = jnp.pad(center, inline_pad)
    along_inline = padded_inline[..., 2:, :, :] + padded_inline[..., :-2, :, :]
    depth_pad = [(0, 0)] * (center.ndim - 1) + [(1, 1)]
    padded_depth = jnp.pad(center, depth_pad)
    along_depth = padded_depth[..., 2:] + padded_depth[..., :-2]
    horizontal = along_inline + along_cross - 4.0 * center
    vertical = along_depth - 2.0 * center
    return (horizontal, vertical)


def diffuse(widened):
    center = widened[..., 1:-1, :]
    inline_pad = [(0, 0)] * (center.ndim - 4) + [(1, 1), (0, 0), (0, 0), (0, 0)]
    padded_inline = jnp.pad(center, inline_pad)
    depth_pad = [(0, 0)] * (center.ndim - 1) + [(1, 1)]
    padded_depth = jnp.pad(center, depth_pad)
    beside_all = [
        padded_inline[..., 2:, :, :, :],
        padded_inline[..., :-2, :, :, :],
        widened[..., 2:, :],
        widened[..., :-2, :],
        padded_depth[..., 2:],
        padded_depth[..., :-2],
    ]
    images = center[..., 0:2, :, :]
    speed_here = center[..., 2:3, :, :]
    totals = jnp.zeros_like(images)
    for beside in beside_all:
        contrast = (beside[..., 2:3, :, :] - speed_here) / EDGE_SCALE
        weight = beside[..., 3:4, :, :] / (1.0 + contrast * contrast)
        totals = totals + weight * (beside[..., 0:2, :, :] - images)
    return images + KAPPA_RATE * totals


def shards(
    speed_blocks,
    aniso_blocks,
    block_owner,
    block_slot,
    state_now,
    state_prev,
    adjoint_now,
    adjoint_prev,
    source_cell,
    wavelet,
    receiver_cell,
    observed,
):
    shot_count = lax.axis_size("shot")
    capacity = 2 * NEED // shot_count
    slots_all = shot_count * capacity
    owners = block_owner[:, 0]
    column_ids = jnp.arange(shot_count, dtype=jnp.int32)
    onehot = (owners[:, None] == column_ids[None, :]).astype(jnp.int32)
    before_count = jnp.sum((jnp.cumsum(onehot, axis=0) - onehot) * onehot, axis=1)
    placed = owners * capacity + before_count
    requests = jnp.full((slots_all,), -1, jnp.int32).at[placed].set(block_slot)
    wanted = lax.all_to_all(
        requests.reshape(shot_count, capacity), "shot", split_axis=0, concat_axis=0, tiled=True
    )
    row_len = speed_blocks.shape[1]
    owned = speed_blocks.shape[0]
    wanted = wanted.reshape(-1)
    owned_rows = jnp.concatenate([speed_blocks, aniso_blocks], axis=1)
    pick = (wanted[:, None] == jnp.arange(owned, dtype=jnp.int32)[None, :]).astype(jnp.float32)
    outgoing = jnp.dot(pick, owned_rows, precision=lax.Precision.HIGHEST)
    incoming = lax.all_to_all(
        outgoing.reshape(shot_count, capacity, 2 * row_len),
        "shot",
        split_axis=0,
        concat_axis=0,
        tiled=True,
    ).reshape(slots_all, 2 * row_len)
    place_hot = (placed[:, None] == jnp.arange(slots_all, dtype=jnp.int32)[None, :]).astype(
        jnp.float32
    )
    fetched = jnp.dot(place_hot, incoming, precision=lax.Precision.HIGHEST)
    grid_dims = state_now.shape
    speeds = fetched[:, :row_len].reshape(grid_dims)
    hfactor = 1.0 + 2.0 * fetched[:, row_len:].reshape(grid_dims)
    previous = state_prev
    current = state_now
    rows_all = grid_dims[0] * grid_dims[1]
    depth = grid_dims[2]
    row_hot = (
        receiver_cell[0][:, None] // depth == jnp.arange(rows_all, dtype=jnp.int32)[None, :]
    ).astype(jnp.float32)
    lane_hot = receiver_cell[0][:, None] % depth == jnp.arange(depth, dtype=jnp.int32)[None, :]
    cell_index = (
        lax.broadcasted_iota(jnp.int32, grid_dims, 0) * (grid_dims[1] * depth)
        + lax.broadcasted_iota(jnp.int32, grid_dims, 1) * depth
        + lax.broadcasted_iota(jnp.int32, grid_dims, 2)
    )
    at_source = cell_index == source_cell[0]
    saved_first = []
    saved_second = []
    misfits = []
    for time_step in range(STEPS):
        horizontal, vertical = curvatures(forward_rims(current))
        advanced = 2.0 * current - previous + speeds * (hfactor * horizontal + vertical)
        advanced = advanced + jnp.where(at_source, wavelet[0, time_step], 0.0)
        picked = jnp.dot(
            row_hot, advanced.reshape(rows_all, depth), precision=lax.Precision.HIGHEST
        )
        synthetic = jnp.sum(jnp.where(lane_hot, picked, 0.0), axis=1)
        misfits.append(synthetic - observed[0, time_step])
        saved_first.append(horizontal)
        saved_second.append(vertical)
        previous, current = (current, advanced)
    later_adjoint = adjoint_prev
    adjoint = adjoint_now
    image_horizontal = jnp.zeros(grid_dims, jnp.float32)
    image_vertical = jnp.zeros(grid_dims, jnp.float32)
    for time_step in range(STEPS - 1, -1, -1):
        horizontal, vertical = curvatures(adjoint_rims_of(adjoint))
        wave_horizontal = saved_first[time_step]
        wave_vertical = saved_second[time_step]
        earlier = 2.0 * adjoint - later_adjoint + speeds * (hfactor * horizontal + vertical)
        spread = jnp.where(lane_hot, misfits[time_step][:, None], 0.0)
        injected = jnp.dot(row_hot.T, spread, precision=lax.Precision.HIGHEST)
        earlier = earlier + injected.reshape(grid_dims)
        image_horizontal = image_horizontal + earlier * wave_horizontal
        image_vertical = image_vertical + earlier * wave_vertical
        later_adjoint, adjoint = (adjoint, earlier)
    gradient_speed = hfactor * image_horizontal + image_vertical
    gradient_aniso = 2.0 * speeds * image_horizontal
    stacked = jnp.stack([gradient_speed, gradient_aniso, speeds, jnp.ones_like(speeds)], axis=1)
    smoothed = diffuse(image_rims_of(stacked))
    rows_out = smoothed.reshape(NEED, 2 * row_len)
    returning = jnp.dot(place_hot.T, rows_out, precision=lax.Precision.HIGHEST)
    returned = lax.all_to_all(
        returning.reshape(shot_count, capacity, 2 * row_len),
        "shot",
        split_axis=0,
        concat_axis=0,
        tiled=True,
    ).reshape(slots_all, 2 * row_len)
    summed = jnp.dot(pick.T, returned, precision=lax.Precision.HIGHEST)
    return (current, (summed * IMAGE_GAIN).reshape(owned, 2, row_len))


def solution(mesh):
    placed = (
        P(("groups", "shot"), None),
        P(("groups", "shot"), None),
        P(("groups", "shot"), None),
        P(("groups", "shot")),
        P(("groups", "shot"), None, None),
        P(("groups", "shot"), None, None),
        P(("groups", "shot"), None, None),
        P(("groups", "shot"), None, None),
        P(("groups", "shot")),
        P(("groups", "shot"), None),
        P(("groups", "shot"), None),
        P(("groups", "shot"), None, None),
    )
    return jax.shard_map(
        shards,
        mesh=mesh,
        in_specs=placed,
        out_specs=(P(("groups", "shot"), None, None), P(("groups", "shot"), None, None)),
        check_vma=False,
    )
```

```python
import jax
import jax.numpy as jnp
from jax import lax
from jax.sharding import PartitionSpec as P

NEED = 128
STEPS = 4
SPLIT = 8


EDGE_SCALE = 0.02
KAPPA_RATE = 0.15
IMAGE_GAIN = 0.03125


def extended(array, sides, width):
    for axis, dim in sides:
        count, length = (lax.axis_size(axis), array.shape[dim])
        joined = [i for i in range(count - 1) if (i + SPLIT // 2) % SPLIT < SPLIT - 1]
        inner = [(i, i + 1) for i in joined if i % 2 == 0]
        outer = [(i, i + 1) for i in joined if i % 2 == 1]
        inner = inner + [(j, i) for i, j in inner]
        outer = outer + [(j, i) for i, j in outer]
        last = lax.slice_in_dim(array, length - width, length, axis=dim)
        leading = lax.slice_in_dim(array, 0, width, axis=dim)
        even = lax.axis_index(axis) % 2 == 0
        got_inner = lax.ppermute(jnp.where(even, last, leading), axis, inner)
        got_outer = lax.ppermute(jnp.where(even, leading, last), axis, outer)
        before = jnp.where(even, got_outer, got_inner)
        after = jnp.where(even, got_inner, got_outer)
        array = jnp.concatenate([before, array, after], axis=dim)
    return array


def cross_mask(widened, axis_at):
    position = (lax.axis_index("shot") + SPLIT // 2) % SPLIT
    extent = widened.shape[axis_at]
    row_index = lax.broadcasted_iota(jnp.int32, (extent,), 0)
    keep_lower = jnp.logical_or(row_index > 0, position > 0)
    keep_upper = jnp.logical_or(row_index < extent - 1, position < SPLIT - 1)
    keep_mask = jnp.logical_and(keep_lower, keep_upper).astype(widened.dtype)
    dims_out = [1] * widened.ndim
    dims_out[axis_at] = extent
    return widened * keep_mask.reshape(dims_out)


def forward_rims(wavefield):
    return cross_mask(extended(wavefield, (("shot", 1),), 1), 1)


def adjoint_rims_of(wavefield):
    return cross_mask(extended(wavefield, (("shot", 1),), 1), 1)


def image_rims_of(stacked):
    return cross_mask(extended(stacked, (("shot", 2),), 1), 2)


def curvatures(widened):
    center = widened[..., 1:-1, :]
    along_cross = widened[..., 2:, :] + widened[..., :-2, :]
    inline_pad = [(0, 0)] * (center.ndim - 3) + [(1, 1), (0, 0), (0, 0)]
    padded_inline = jnp.pad(center, inline_pad)
    along_inline = padded_inline[..., 2:, :, :] + padded_inline[..., :-2, :, :]
    depth_pad = [(0, 0)] * (center.ndim - 1) + [(1, 1)]
    padded_depth = jnp.pad(center, depth_pad)
    along_depth = padded_depth[..., 2:] + padded_depth[..., :-2]
    horizontal = along_inline + along_cross - 4.0 * center
    vertical = along_depth - 2.0 * center
    return (horizontal, vertical)


def diffuse(widened):
    center = widened[..., 1:-1, :]
    inline_pad = [(0, 0)] * (center.ndim - 4) + [(1, 1), (0, 0), (0, 0), (0, 0)]
    padded_inline = jnp.pad(center, inline_pad)
    depth_pad = [(0, 0)] * (center.ndim - 1) + [(1, 1)]
    padded_depth = jnp.pad(center, depth_pad)
    beside_all = [
        padded_inline[..., 2:, :, :, :],
        padded_inline[..., :-2, :, :, :],
        widened[..., 2:, :],
        widened[..., :-2, :],
        padded_depth[..., 2:],
        padded_depth[..., :-2],
    ]
    images = center[..., 0:2, :, :]
    speed_here = center[..., 2:3, :, :]
    totals = jnp.zeros_like(images)
    for beside in beside_all:
        contrast = (beside[..., 2:3, :, :] - speed_here) / EDGE_SCALE
        weight = beside[..., 3:4, :, :] / (1.0 + contrast * contrast)
        totals = totals + weight * (beside[..., 0:2, :, :] - images)
    return images + KAPPA_RATE * totals


def split3(x):
    hi = lax.reduce_precision(x, exponent_bits=8, mantissa_bits=7)
    rest = x - hi
    mid = lax.reduce_precision(rest, exponent_bits=8, mantissa_bits=7)
    lo = rest - mid
    return jnp.concatenate([hi, mid, lo], axis=-1).astype(jnp.bfloat16)


def select_dot(hot, values):
    width = values.shape[-1]
    out = jnp.dot(hot.astype(jnp.bfloat16), split3(values), preferred_element_type=jnp.float32)
    return (out[:, :width] + out[:, width : 2 * width]) + out[:, 2 * width :]


def shards(
    speed_blocks,
    aniso_blocks,
    block_owner,
    block_slot,
    state_now,
    state_prev,
    adjoint_now,
    adjoint_prev,
    source_cell,
    wavelet,
    receiver_cell,
    observed,
):
    shot_count = lax.axis_size("shot")
    capacity = 2 * NEED // shot_count
    slots_all = shot_count * capacity
    owners = block_owner[:, 0]
    column_ids = jnp.arange(shot_count, dtype=jnp.int32)
    onehot = (owners[:, None] == column_ids[None, :]).astype(jnp.int32)
    before_count = jnp.sum((jnp.cumsum(onehot, axis=0) - onehot) * onehot, axis=1)
    placed = owners * capacity + before_count
    requests = jnp.full((slots_all,), -1, jnp.int32).at[placed].set(block_slot)
    wanted = lax.all_to_all(
        requests.reshape(shot_count, capacity), "shot", split_axis=0, concat_axis=0, tiled=True
    )
    row_len = speed_blocks.shape[1]
    owned = speed_blocks.shape[0]
    wanted = wanted.reshape(-1)
    owned_rows = jnp.concatenate([speed_blocks, aniso_blocks], axis=1)
    pick = (wanted[:, None] == jnp.arange(owned, dtype=jnp.int32)[None, :]).astype(jnp.float32)
    outgoing = jnp.dot(pick, owned_rows, precision=lax.Precision.HIGHEST)
    incoming = lax.all_to_all(
        outgoing.reshape(shot_count, capacity, 2 * row_len),
        "shot",
        split_axis=0,
        concat_axis=0,
        tiled=True,
    ).reshape(slots_all, 2 * row_len)
    place_hot = (placed[:, None] == jnp.arange(slots_all, dtype=jnp.int32)[None, :]).astype(
        jnp.float32
    )
    fetched = jnp.dot(place_hot, incoming, precision=lax.Precision.HIGHEST)
    grid_dims = state_now.shape
    speeds = fetched[:, :row_len].reshape(grid_dims)
    hfactor = 1.0 + 2.0 * fetched[:, row_len:].reshape(grid_dims)
    previous = state_prev
    current = state_now
    rows_all = grid_dims[0] * grid_dims[1]
    depth = grid_dims[2]
    row_hot = (
        receiver_cell[0][:, None] // depth == jnp.arange(rows_all, dtype=jnp.int32)[None, :]
    ).astype(jnp.float32)
    lane_hot = receiver_cell[0][:, None] % depth == jnp.arange(depth, dtype=jnp.int32)[None, :]
    cell_index = (
        lax.broadcasted_iota(jnp.int32, grid_dims, 0) * (grid_dims[1] * depth)
        + lax.broadcasted_iota(jnp.int32, grid_dims, 1) * depth
        + lax.broadcasted_iota(jnp.int32, grid_dims, 2)
    )
    at_source = cell_index == source_cell[0]
    saved_first = []
    saved_second = []
    misfits = []
    for time_step in range(STEPS):
        horizontal, vertical = curvatures(forward_rims(current))
        advanced = 2.0 * current - previous + speeds * (hfactor * horizontal + vertical)
        advanced = advanced + jnp.where(at_source, wavelet[0, time_step], 0.0)
        picked = select_dot(row_hot, advanced.reshape(rows_all, depth))
        synthetic = jnp.sum(jnp.where(lane_hot, picked, 0.0), axis=1)
        misfits.append(synthetic - observed[0, time_step])
        saved_first.append(horizontal)
        saved_second.append(vertical)
        previous, current = (current, advanced)
    later_adjoint = adjoint_prev
    adjoint = adjoint_now
    image_horizontal = jnp.zeros(grid_dims, jnp.float32)
    image_vertical = jnp.zeros(grid_dims, jnp.float32)
    for time_step in range(STEPS - 1, -1, -1):
        horizontal, vertical = curvatures(adjoint_rims_of(adjoint))
        wave_horizontal = saved_first[time_step]
        wave_vertical = saved_second[time_step]
        earlier = 2.0 * adjoint - later_adjoint + speeds * (hfactor * horizontal + vertical)
        spread = jnp.where(lane_hot, misfits[time_step][:, None], 0.0)
        injected = select_dot(row_hot.T, spread)
        earlier = earlier + injected.reshape(grid_dims)
        image_horizontal = image_horizontal + earlier * wave_horizontal
        image_vertical = image_vertical + earlier * wave_vertical
        later_adjoint, adjoint = (adjoint, earlier)
    gradient_speed = hfactor * image_horizontal + image_vertical
    gradient_aniso = 2.0 * speeds * image_horizontal
    stacked = jnp.stack([gradient_speed, gradient_aniso, speeds, jnp.ones_like(speeds)], axis=1)
    smoothed = diffuse(image_rims_of(stacked))
    rows_out = smoothed.reshape(NEED, 2 * row_len)
    returning = jnp.dot(place_hot.T, rows_out, precision=lax.Precision.HIGHEST)
    returned = lax.all_to_all(
        returning.reshape(shot_count, capacity, 2 * row_len),
        "shot",
        split_axis=0,
        concat_axis=0,
        tiled=True,
    ).reshape(slots_all, 2 * row_len)
    summed = jnp.dot(pick.T, returned, precision=lax.Precision.HIGHEST)
    return (current, (summed * IMAGE_GAIN).reshape(owned, 2, row_len))


def solution(mesh):
    placed = (
        P(("groups", "shot"), None),
        P(("groups", "shot"), None),
        P(("groups", "shot"), None),
        P(("groups", "shot")),
        P(("groups", "shot"), None, None),
        P(("groups", "shot"), None, None),
        P(("groups", "shot"), None, None),
        P(("groups", "shot"), None, None),
        P(("groups", "shot")),
        P(("groups", "shot"), None),
        P(("groups", "shot"), None),
        P(("groups", "shot"), None, None),
    )
    return jax.shard_map(
        shards,
        mesh=mesh,
        in_specs=placed,
        out_specs=(P(("groups", "shot"), None, None), P(("groups", "shot"), None, None)),
        check_vma=False,
    )
```

```python
import jax
import jax.numpy as jnp
from jax import lax
from jax.sharding import PartitionSpec as P

NEED = 128
STEPS = 4
SPLIT = 8


EDGE_SCALE = 0.02
KAPPA_RATE = 0.15
IMAGE_GAIN = 0.03125


def extended(array, sides, width):
    for axis, dim in sides:
        count, length = (lax.axis_size(axis), array.shape[dim])
        joined = [i for i in range(count - 1) if (i + SPLIT // 2) % SPLIT < SPLIT - 1]
        inner = [(i, i + 1) for i in joined if i % 2 == 0]
        outer = [(i, i + 1) for i in joined if i % 2 == 1]
        inner = inner + [(j, i) for i, j in inner]
        outer = outer + [(j, i) for i, j in outer]
        last = lax.slice_in_dim(array, length - width, length, axis=dim)
        leading = lax.slice_in_dim(array, 0, width, axis=dim)
        even = lax.axis_index(axis) % 2 == 0
        got_inner = lax.ppermute(jnp.where(even, last, leading), axis, inner)
        got_outer = lax.ppermute(jnp.where(even, leading, last), axis, outer)
        before = jnp.where(even, got_outer, got_inner)
        after = jnp.where(even, got_inner, got_outer)
        array = jnp.concatenate([before, array, after], axis=dim)
    return array


def cross_mask(widened, axis_at):
    position = (lax.axis_index("shot") + SPLIT // 2) % SPLIT
    extent = widened.shape[axis_at]
    row_index = lax.broadcasted_iota(jnp.int32, (extent,), 0)
    keep_lower = jnp.logical_or(row_index > 0, position > 0)
    keep_upper = jnp.logical_or(row_index < extent - 1, position < SPLIT - 1)
    keep_mask = jnp.logical_and(keep_lower, keep_upper).astype(widened.dtype)
    dims_out = [1] * widened.ndim
    dims_out[axis_at] = extent
    return widened * keep_mask.reshape(dims_out)


def forward_rims(wavefield):
    return cross_mask(extended(wavefield, (("shot", 1),), 1), 1)


def adjoint_rims_of(wavefield):
    return cross_mask(extended(wavefield, (("shot", 1),), 1), 1)


def image_rims_of(stacked):
    return cross_mask(extended(stacked, (("shot", 2),), 1), 2)


def curvatures(widened):
    center = widened[..., 1:-1, :]
    along_cross = widened[..., 2:, :] + widened[..., :-2, :]
    inline_pad = [(0, 0)] * (center.ndim - 3) + [(1, 1), (0, 0), (0, 0)]
    padded_inline = jnp.pad(center, inline_pad)
    along_inline = padded_inline[..., 2:, :, :] + padded_inline[..., :-2, :, :]
    depth_pad = [(0, 0)] * (center.ndim - 1) + [(1, 1)]
    padded_depth = jnp.pad(center, depth_pad)
    along_depth = padded_depth[..., 2:] + padded_depth[..., :-2]
    horizontal = along_inline + along_cross - 4.0 * center
    vertical = along_depth - 2.0 * center
    return (horizontal, vertical)


def diffuse(widened):
    center = widened[..., 1:-1, :]
    inline_pad = [(0, 0)] * (center.ndim - 4) + [(1, 1), (0, 0), (0, 0), (0, 0)]
    padded_inline = jnp.pad(center, inline_pad)
    depth_pad = [(0, 0)] * (center.ndim - 1) + [(1, 1)]
    padded_depth = jnp.pad(center, depth_pad)
    beside_all = [
        padded_inline[..., 2:, :, :, :],
        padded_inline[..., :-2, :, :, :],
        widened[..., 2:, :],
        widened[..., :-2, :],
        padded_depth[..., 2:],
        padded_depth[..., :-2],
    ]
    images = center[..., 0:2, :, :]
    speed_here = center[..., 2:3, :, :]
    totals = jnp.zeros_like(images)
    for beside in beside_all:
        contrast = (beside[..., 2:3, :, :] - speed_here) / EDGE_SCALE
        weight = beside[..., 3:4, :, :] / (1.0 + contrast * contrast)
        totals = totals + weight * (beside[..., 0:2, :, :] - images)
    return images + KAPPA_RATE * totals


def split3(x):
    hi = lax.reduce_precision(x, exponent_bits=8, mantissa_bits=7)
    rest = x - hi
    mid = lax.reduce_precision(rest, exponent_bits=8, mantissa_bits=7)
    lo = rest - mid
    return jnp.concatenate([hi, mid, lo], axis=-1).astype(jnp.bfloat16)


def select_dot(hot, values):
    width = values.shape[-1]
    out = jnp.dot(hot.astype(jnp.bfloat16), split3(values), preferred_element_type=jnp.float32)
    return (out[:, :width] + out[:, width : 2 * width]) + out[:, 2 * width :]


def shards(
    speed_blocks,
    aniso_blocks,
    block_owner,
    block_slot,
    state_now,
    state_prev,
    adjoint_now,
    adjoint_prev,
    source_cell,
    wavelet,
    receiver_cell,
    observed,
):
    shot_count = lax.axis_size("shot")
    capacity = 2 * NEED // shot_count
    slots_all = shot_count * capacity
    owners = block_owner[:, 0]
    column_ids = jnp.arange(shot_count, dtype=jnp.int32)
    onehot = (owners[:, None] == column_ids[None, :]).astype(jnp.int32)
    before_count = jnp.sum((jnp.cumsum(onehot, axis=0) - onehot) * onehot, axis=1)
    placed = owners * capacity + before_count
    requests = jnp.full((slots_all,), -1, jnp.int32).at[placed].set(block_slot)
    wanted = lax.all_to_all(
        requests.reshape(shot_count, capacity), "shot", split_axis=0, concat_axis=0, tiled=True
    )
    row_len = speed_blocks.shape[1]
    owned = speed_blocks.shape[0]
    wanted = wanted.reshape(-1)
    owned_rows = jnp.concatenate([speed_blocks, aniso_blocks], axis=1)
    pick = (wanted[:, None] == jnp.arange(owned, dtype=jnp.int32)[None, :]).astype(jnp.float32)
    outgoing = jnp.dot(pick, owned_rows, precision=lax.Precision.HIGHEST)
    incoming = lax.all_to_all(
        outgoing.reshape(shot_count, capacity, 2 * row_len),
        "shot",
        split_axis=0,
        concat_axis=0,
        tiled=True,
    ).reshape(slots_all, 2 * row_len)
    place_hot = (placed[:, None] == jnp.arange(slots_all, dtype=jnp.int32)[None, :]).astype(
        jnp.float32
    )
    fetched = jnp.dot(place_hot, incoming, precision=lax.Precision.HIGHEST)
    grid_dims = state_now.shape
    speeds = fetched[:, :row_len].reshape(grid_dims)
    hfactor = 1.0 + 2.0 * fetched[:, row_len:].reshape(grid_dims)
    previous = state_prev
    current = state_now
    rows_all = grid_dims[0] * grid_dims[1]
    depth = grid_dims[2]
    row_hot = (
        receiver_cell[0][:, None] // depth == jnp.arange(rows_all, dtype=jnp.int32)[None, :]
    ).astype(jnp.float32)
    lane_hot = receiver_cell[0][:, None] % depth == jnp.arange(depth, dtype=jnp.int32)[None, :]
    cell_index = (
        lax.broadcasted_iota(jnp.int32, grid_dims, 0) * (grid_dims[1] * depth)
        + lax.broadcasted_iota(jnp.int32, grid_dims, 1) * depth
        + lax.broadcasted_iota(jnp.int32, grid_dims, 2)
    )
    at_source = cell_index == source_cell[0]
    saved_first = []
    saved_second = []
    misfits = []
    for time_step in range(STEPS):
        horizontal, vertical = curvatures(forward_rims(current))
        advanced = 2.0 * current - previous + speeds * (hfactor * horizontal + vertical)
        advanced = advanced + jnp.where(at_source, wavelet[0, time_step], 0.0)
        picked = select_dot(row_hot, advanced.reshape(rows_all, depth))
        synthetic = jnp.sum(jnp.where(lane_hot, picked, 0.0), axis=1)
        misfits.append(synthetic - observed[0, time_step])
        saved_first.append(horizontal)
        saved_second.append(vertical)
        previous, current = (current, advanced)
    later_adjoint = adjoint_prev
    adjoint = adjoint_now
    image_horizontal = jnp.zeros(grid_dims, jnp.float32)
    image_vertical = jnp.zeros(grid_dims, jnp.float32)
    for time_step in range(STEPS - 1, -1, -1):
        horizontal, vertical = curvatures(adjoint_rims_of(adjoint))
        wave_horizontal = saved_first[time_step]
        wave_vertical = saved_second[time_step]
        earlier = 2.0 * adjoint - later_adjoint + speeds * (hfactor * horizontal + vertical)
        spread = jnp.where(lane_hot, misfits[time_step][:, None], 0.0)
        injected = select_dot(row_hot.T, spread)
        earlier = earlier + injected.reshape(grid_dims)
        image_horizontal = image_horizontal + earlier * wave_horizontal
        image_vertical = image_vertical + earlier * wave_vertical
        later_adjoint, adjoint = (adjoint, earlier)
    gradient_speed = hfactor * image_horizontal + image_vertical
    gradient_aniso = 2.0 * speeds * image_horizontal
    stacked = jnp.stack([gradient_speed, gradient_aniso, speeds, jnp.ones_like(speeds)], axis=1)
    smoothed = diffuse(image_rims_of(stacked))
    rows_out = smoothed.reshape(NEED, 2 * row_len)
    returning = select_dot(place_hot.T, rows_out)
    returned = lax.all_to_all(
        returning.reshape(shot_count, capacity, 2 * row_len),
        "shot",
        split_axis=0,
        concat_axis=0,
        tiled=True,
    ).reshape(slots_all, 2 * row_len)
    summed = jnp.dot(pick.T, returned, precision=lax.Precision.HIGHEST)
    return (current, (summed * IMAGE_GAIN).reshape(owned, 2, row_len))


def solution(mesh):
    placed = (
        P(("groups", "shot"), None),
        P(("groups", "shot"), None),
        P(("groups", "shot"), None),
        P(("groups", "shot")),
        P(("groups", "shot"), None, None),
        P(("groups", "shot"), None, None),
        P(("groups", "shot"), None, None),
        P(("groups", "shot"), None, None),
        P(("groups", "shot")),
        P(("groups", "shot"), None),
        P(("groups", "shot"), None),
        P(("groups", "shot"), None, None),
    )
    return jax.shard_map(
        shards,
        mesh=mesh,
        in_specs=placed,
        out_specs=(P(("groups", "shot"), None, None), P(("groups", "shot"), None, None)),
        check_vma=False,
    )
```

```python
import jax
import jax.numpy as jnp
from jax import lax
from jax.sharding import PartitionSpec as P

NEED = 128
STEPS = 4
SPLIT = 8


EDGE_SCALE = 0.02
KAPPA_RATE = 0.15
IMAGE_GAIN = 0.03125


def extended(array, sides, width):
    for axis, dim in sides:
        count, length = (lax.axis_size(axis), array.shape[dim])
        joined = [i for i in range(count - 1) if (i + SPLIT // 2) % SPLIT < SPLIT - 1]
        inner = [(i, i + 1) for i in joined if i % 2 == 0]
        outer = [(i, i + 1) for i in joined if i % 2 == 1]
        inner = inner + [(j, i) for i, j in inner]
        outer = outer + [(j, i) for i, j in outer]
        last = lax.slice_in_dim(array, length - width, length, axis=dim)
        leading = lax.slice_in_dim(array, 0, width, axis=dim)
        even = lax.axis_index(axis) % 2 == 0
        got_inner = lax.ppermute(jnp.where(even, last, leading), axis, inner)
        got_outer = lax.ppermute(jnp.where(even, leading, last), axis, outer)
        before = jnp.where(even, got_outer, got_inner)
        after = jnp.where(even, got_inner, got_outer)
        array = jnp.concatenate([before, array, after], axis=dim)
    return array


def cross_mask(widened, axis_at):
    position = (lax.axis_index("shot") + SPLIT // 2) % SPLIT
    extent = widened.shape[axis_at]
    row_index = lax.broadcasted_iota(jnp.int32, (extent,), 0)
    keep_lower = jnp.logical_or(row_index > 0, position > 0)
    keep_upper = jnp.logical_or(row_index < extent - 1, position < SPLIT - 1)
    keep_mask = jnp.logical_and(keep_lower, keep_upper).astype(widened.dtype)
    dims_out = [1] * widened.ndim
    dims_out[axis_at] = extent
    return widened * keep_mask.reshape(dims_out)


def forward_rims(wavefield):
    return cross_mask(extended(wavefield, (("shot", 1),), 1), 1)


def adjoint_rims_of(wavefield):
    return cross_mask(extended(wavefield, (("shot", 1),), 1), 1)


def image_rims_of(stacked):
    return cross_mask(extended(stacked, (("shot", 2),), 1), 2)


def curvatures(widened):
    center = widened[..., 1:-1, :]
    along_cross = widened[..., 2:, :] + widened[..., :-2, :]
    inline_pad = [(0, 0)] * (center.ndim - 3) + [(1, 1), (0, 0), (0, 0)]
    padded_inline = jnp.pad(center, inline_pad)
    along_inline = padded_inline[..., 2:, :, :] + padded_inline[..., :-2, :, :]
    depth_pad = [(0, 0)] * (center.ndim - 1) + [(1, 1)]
    padded_depth = jnp.pad(center, depth_pad)
    along_depth = padded_depth[..., 2:] + padded_depth[..., :-2]
    horizontal = along_inline + along_cross - 4.0 * center
    vertical = along_depth - 2.0 * center
    return (horizontal, vertical)


def diffuse(widened):
    center = widened[..., 1:-1, :]
    inline_pad = [(0, 0)] * (center.ndim - 4) + [(1, 1), (0, 0), (0, 0), (0, 0)]
    padded_inline = jnp.pad(center, inline_pad)
    depth_pad = [(0, 0)] * (center.ndim - 1) + [(1, 1)]
    padded_depth = jnp.pad(center, depth_pad)
    beside_all = [
        padded_inline[..., 2:, :, :, :],
        padded_inline[..., :-2, :, :, :],
        widened[..., 2:, :],
        widened[..., :-2, :],
        padded_depth[..., 2:],
        padded_depth[..., :-2],
    ]
    images = center[..., 0:2, :, :]
    speed_here = center[..., 2:3, :, :]
    totals = jnp.zeros_like(images)
    for beside in beside_all:
        contrast = (beside[..., 2:3, :, :] - speed_here) / EDGE_SCALE
        weight = beside[..., 3:4, :, :] / (1.0 + contrast * contrast)
        totals = totals + weight * (beside[..., 0:2, :, :] - images)
    return images + KAPPA_RATE * totals


def split3(x):
    hi = lax.reduce_precision(x, exponent_bits=8, mantissa_bits=7)
    rest = x - hi
    mid = lax.reduce_precision(rest, exponent_bits=8, mantissa_bits=7)
    lo = rest - mid
    return jnp.concatenate([hi, mid, lo], axis=-1).astype(jnp.bfloat16)


def select_dot(hot, values):
    width = values.shape[-1]
    out = jnp.dot(hot.astype(jnp.bfloat16), split3(values), preferred_element_type=jnp.float32)
    return (out[:, :width] + out[:, width : 2 * width]) + out[:, 2 * width :]


def shards(
    speed_blocks,
    aniso_blocks,
    block_owner,
    block_slot,
    state_now,
    state_prev,
    adjoint_now,
    adjoint_prev,
    source_cell,
    wavelet,
    receiver_cell,
    observed,
):
    shot_count = lax.axis_size("shot")
    capacity = 2 * NEED // shot_count
    slots_all = shot_count * capacity
    owners = block_owner[:, 0]
    column_ids = jnp.arange(shot_count, dtype=jnp.int32)
    onehot = (owners[:, None] == column_ids[None, :]).astype(jnp.int32)
    before_count = jnp.sum((jnp.cumsum(onehot, axis=0) - onehot) * onehot, axis=1)
    placed = owners * capacity + before_count
    requests = jnp.full((slots_all,), -1, jnp.int32).at[placed].set(block_slot)
    wanted = lax.all_to_all(
        requests.reshape(shot_count, capacity), "shot", split_axis=0, concat_axis=0, tiled=True
    )
    row_len = speed_blocks.shape[1]
    owned = speed_blocks.shape[0]
    wanted = wanted.reshape(-1)
    owned_rows = jnp.concatenate([speed_blocks, aniso_blocks], axis=1)
    pick = (wanted[:, None] == jnp.arange(owned, dtype=jnp.int32)[None, :]).astype(jnp.float32)
    outgoing = jnp.dot(pick, owned_rows, precision=lax.Precision.HIGHEST)
    incoming = lax.all_to_all(
        outgoing.reshape(shot_count, capacity, 2 * row_len),
        "shot",
        split_axis=0,
        concat_axis=0,
        tiled=True,
    ).reshape(slots_all, 2 * row_len)
    place_hot = (placed[:, None] == jnp.arange(slots_all, dtype=jnp.int32)[None, :]).astype(
        jnp.float32
    )
    fetched = jnp.dot(place_hot, incoming, precision=lax.Precision.HIGHEST)
    grid_dims = state_now.shape
    speeds = fetched[:, :row_len].reshape(grid_dims)
    hfactor = 1.0 + 2.0 * fetched[:, row_len:].reshape(grid_dims)
    previous = state_prev
    current = state_now
    rows_all = grid_dims[0] * grid_dims[1]
    depth = grid_dims[2]
    row_hot = (
        receiver_cell[0][:, None] // depth == jnp.arange(rows_all, dtype=jnp.int32)[None, :]
    ).astype(jnp.float32)
    lane_hot = receiver_cell[0][:, None] % depth == jnp.arange(depth, dtype=jnp.int32)[None, :]
    cell_index = (
        lax.broadcasted_iota(jnp.int32, grid_dims, 0) * (grid_dims[1] * depth)
        + lax.broadcasted_iota(jnp.int32, grid_dims, 1) * depth
        + lax.broadcasted_iota(jnp.int32, grid_dims, 2)
    )
    at_source = cell_index == source_cell[0]
    saved_first = []
    saved_second = []
    misfits = []
    for time_step in range(STEPS):
        horizontal, vertical = curvatures(forward_rims(current))
        advanced = 2.0 * current - previous + speeds * (hfactor * horizontal + vertical)
        advanced = advanced + jnp.where(at_source, wavelet[0, time_step], 0.0)
        picked = select_dot(row_hot, advanced.reshape(rows_all, depth))
        synthetic = jnp.sum(jnp.where(lane_hot, picked, 0.0), axis=1)
        misfits.append(synthetic - observed[0, time_step])
        saved_first.append(horizontal)
        saved_second.append(vertical)
        previous, current = (current, advanced)
    later_adjoint = adjoint_prev
    adjoint = adjoint_now
    image_horizontal = jnp.zeros(grid_dims, jnp.float32)
    image_vertical = jnp.zeros(grid_dims, jnp.float32)
    for time_step in range(STEPS - 1, -1, -1):
        horizontal, vertical = curvatures(adjoint_rims_of(adjoint))
        wave_horizontal = saved_first[time_step]
        wave_vertical = saved_second[time_step]
        earlier = 2.0 * adjoint - later_adjoint + speeds * (hfactor * horizontal + vertical)
        spread = jnp.where(lane_hot, misfits[time_step][:, None], 0.0)
        injected = select_dot(row_hot.T, spread)
        earlier = earlier + injected.reshape(grid_dims)
        image_horizontal = image_horizontal + earlier * wave_horizontal
        image_vertical = image_vertical + earlier * wave_vertical
        later_adjoint, adjoint = (adjoint, earlier)
    gradient_speed = hfactor * image_horizontal + image_vertical
    gradient_aniso = 2.0 * speeds * image_horizontal
    stacked = jnp.stack([gradient_speed, gradient_aniso, speeds], axis=1)
    widened = image_rims_of(stacked)
    me = lax.axis_index("shot")
    position = (me + SPLIT // 2) % SPLIT
    layer = lax.broadcasted_iota(jnp.int32, (1, 1, widened.shape[2], 1), 2)
    has_below = jnp.logical_and(position > 0, me > 0)
    has_above = jnp.logical_and(position < SPLIT - 1, me < shot_count - 1)
    exists = jnp.where(layer == 0, has_below, jnp.where(layer == widened.shape[2] - 1, has_above, True))
    ones = jnp.broadcast_to(exists.astype(jnp.float32), widened[:, :1].shape)
    smoothed = diffuse(jnp.concatenate([widened, ones], axis=1))
    rows_out = smoothed.reshape(NEED, 2 * row_len)
    returning = jnp.dot(place_hot.T, rows_out, precision=lax.Precision.HIGHEST)
    returned = lax.all_to_all(
        returning.reshape(shot_count, capacity, 2 * row_len),
        "shot",
        split_axis=0,
        concat_axis=0,
        tiled=True,
    ).reshape(slots_all, 2 * row_len)
    summed = jnp.dot(pick.T, returned, precision=lax.Precision.HIGHEST)
    return (current, (summed * IMAGE_GAIN).reshape(owned, 2, row_len))


def solution(mesh):
    placed = (
        P(("groups", "shot"), None),
        P(("groups", "shot"), None),
        P(("groups", "shot"), None),
        P(("groups", "shot")),
        P(("groups", "shot"), None, None),
        P(("groups", "shot"), None, None),
        P(("groups", "shot"), None, None),
        P(("groups", "shot"), None, None),
        P(("groups", "shot")),
        P(("groups", "shot"), None),
        P(("groups", "shot"), None),
        P(("groups", "shot"), None, None),
    )
    return jax.shard_map(
        shards,
        mesh=mesh,
        in_specs=placed,
        out_specs=(P(("groups", "shot"), None, None), P(("groups", "shot"), None, None)),
        check_vma=False,
    )
```

```python
import jax
import jax.numpy as jnp
from jax import lax
from jax.sharding import PartitionSpec as P

NEED = 128
STEPS = 4
SPLIT = 8


EDGE_SCALE = 0.02
KAPPA_RATE = 0.15
IMAGE_GAIN = 0.03125


def extended(array, sides, width):
    for axis, dim in sides:
        count, length = (lax.axis_size(axis), array.shape[dim])
        joined = [i for i in range(count - 1) if (i + SPLIT // 2) % SPLIT < SPLIT - 1]
        inner = [(i, i + 1) for i in joined if i % 2 == 0]
        outer = [(i, i + 1) for i in joined if i % 2 == 1]
        inner = inner + [(j, i) for i, j in inner]
        outer = outer + [(j, i) for i, j in outer]
        last = lax.slice_in_dim(array, length - width, length, axis=dim)
        leading = lax.slice_in_dim(array, 0, width, axis=dim)
        even = lax.axis_index(axis) % 2 == 0
        got_inner = lax.ppermute(jnp.where(even, last, leading), axis, inner)
        got_outer = lax.ppermute(jnp.where(even, leading, last), axis, outer)
        before = jnp.where(even, got_outer, got_inner)
        after = jnp.where(even, got_inner, got_outer)
        array = jnp.concatenate([before, array, after], axis=dim)
    return array


def cross_mask(widened, axis_at):
    position = (lax.axis_index("shot") + SPLIT // 2) % SPLIT
    extent = widened.shape[axis_at]
    row_index = lax.broadcasted_iota(jnp.int32, (extent,), 0)
    keep_lower = jnp.logical_or(row_index > 0, position > 0)
    keep_upper = jnp.logical_or(row_index < extent - 1, position < SPLIT - 1)
    keep_mask = jnp.logical_and(keep_lower, keep_upper).astype(widened.dtype)
    dims_out = [1] * widened.ndim
    dims_out[axis_at] = extent
    return widened * keep_mask.reshape(dims_out)


def forward_rims(wavefield):
    return extended(wavefield, (("shot", 1),), 1)


def adjoint_rims_of(wavefield):
    return extended(wavefield, (("shot", 1),), 1)


def image_rims_of(stacked):
    return extended(stacked, (("shot", 2),), 1)


def curvatures(widened):
    center = widened[..., 1:-1, :]
    along_cross = widened[..., 2:, :] + widened[..., :-2, :]
    inline_pad = [(0, 0)] * (center.ndim - 3) + [(1, 1), (0, 0), (0, 0)]
    padded_inline = jnp.pad(center, inline_pad)
    along_inline = padded_inline[..., 2:, :, :] + padded_inline[..., :-2, :, :]
    depth_pad = [(0, 0)] * (center.ndim - 1) + [(1, 1)]
    padded_depth = jnp.pad(center, depth_pad)
    along_depth = padded_depth[..., 2:] + padded_depth[..., :-2]
    horizontal = along_inline + along_cross - 4.0 * center
    vertical = along_depth - 2.0 * center
    return (horizontal, vertical)


def diffuse(widened):
    center = widened[..., 1:-1, :]
    inline_pad = [(0, 0)] * (center.ndim - 4) + [(1, 1), (0, 0), (0, 0), (0, 0)]
    padded_inline = jnp.pad(center, inline_pad)
    depth_pad = [(0, 0)] * (center.ndim - 1) + [(1, 1)]
    padded_depth = jnp.pad(center, depth_pad)
    beside_all = [
        padded_inline[..., 2:, :, :, :],
        padded_inline[..., :-2, :, :, :],
        widened[..., 2:, :],
        widened[..., :-2, :],
        padded_depth[..., 2:],
        padded_depth[..., :-2],
    ]
    images = center[..., 0:2, :, :]
    speed_here = center[..., 2:3, :, :]
    totals = jnp.zeros_like(images)
    for beside in beside_all:
        contrast = (beside[..., 2:3, :, :] - speed_here) / EDGE_SCALE
        weight = beside[..., 3:4, :, :] / (1.0 + contrast * contrast)
        totals = totals + weight * (beside[..., 0:2, :, :] - images)
    return images + KAPPA_RATE * totals


def split3(x):
    hi = lax.reduce_precision(x, exponent_bits=8, mantissa_bits=7)
    rest = x - hi
    mid = lax.reduce_precision(rest, exponent_bits=8, mantissa_bits=7)
    lo = rest - mid
    return jnp.concatenate([hi, mid, lo], axis=-1).astype(jnp.bfloat16)


def select_dot(hot, values):
    width = values.shape[-1]
    out = jnp.dot(hot.astype(jnp.bfloat16), split3(values), preferred_element_type=jnp.float32)
    return (out[:, :width] + out[:, width : 2 * width]) + out[:, 2 * width :]


def shards(
    speed_blocks,
    aniso_blocks,
    block_owner,
    block_slot,
    state_now,
    state_prev,
    adjoint_now,
    adjoint_prev,
    source_cell,
    wavelet,
    receiver_cell,
    observed,
):
    shot_count = lax.axis_size("shot")
    capacity = 2 * NEED // shot_count
    slots_all = shot_count * capacity
    owners = block_owner[:, 0]
    column_ids = jnp.arange(shot_count, dtype=jnp.int32)
    onehot = (owners[:, None] == column_ids[None, :]).astype(jnp.int32)
    before_count = jnp.sum((jnp.cumsum(onehot, axis=0) - onehot) * onehot, axis=1)
    placed = owners * capacity + before_count
    requests = jnp.full((slots_all,), -1, jnp.int32).at[placed].set(block_slot)
    wanted = lax.all_to_all(
        requests.reshape(shot_count, capacity), "shot", split_axis=0, concat_axis=0, tiled=True
    )
    row_len = speed_blocks.shape[1]
    owned = speed_blocks.shape[0]
    wanted = wanted.reshape(-1)
    owned_rows = jnp.concatenate([speed_blocks, aniso_blocks], axis=1)
    pick = (wanted[:, None] == jnp.arange(owned, dtype=jnp.int32)[None, :]).astype(jnp.float32)
    outgoing = jnp.dot(pick, owned_rows, precision=lax.Precision.HIGHEST)
    incoming = lax.all_to_all(
        outgoing.reshape(shot_count, capacity, 2 * row_len),
        "shot",
        split_axis=0,
        concat_axis=0,
        tiled=True,
    ).reshape(slots_all, 2 * row_len)
    place_hot = (placed[:, None] == jnp.arange(slots_all, dtype=jnp.int32)[None, :]).astype(
        jnp.float32
    )
    fetched = jnp.dot(place_hot, incoming, precision=lax.Precision.HIGHEST)
    grid_dims = state_now.shape
    speeds = fetched[:, :row_len].reshape(grid_dims)
    hfactor = 1.0 + 2.0 * fetched[:, row_len:].reshape(grid_dims)
    previous = state_prev
    current = state_now
    rows_all = grid_dims[0] * grid_dims[1]
    depth = grid_dims[2]
    row_hot = (
        receiver_cell[0][:, None] // depth == jnp.arange(rows_all, dtype=jnp.int32)[None, :]
    ).astype(jnp.float32)
    lane_hot = receiver_cell[0][:, None] % depth == jnp.arange(depth, dtype=jnp.int32)[None, :]
    cell_index = (
        lax.broadcasted_iota(jnp.int32, grid_dims, 0) * (grid_dims[1] * depth)
        + lax.broadcasted_iota(jnp.int32, grid_dims, 1) * depth
        + lax.broadcasted_iota(jnp.int32, grid_dims, 2)
    )
    at_source = cell_index == source_cell[0]
    saved_first = []
    saved_second = []
    misfits = []
    for time_step in range(STEPS):
        horizontal, vertical = curvatures(forward_rims(current))
        advanced = 2.0 * current - previous + speeds * (hfactor * horizontal + vertical)
        advanced = advanced + jnp.where(at_source, wavelet[0, time_step], 0.0)
        picked = select_dot(row_hot, advanced.reshape(rows_all, depth))
        synthetic = jnp.sum(jnp.where(lane_hot, picked, 0.0), axis=1)
        misfits.append(synthetic - observed[0, time_step])
        saved_first.append(horizontal)
        saved_second.append(vertical)
        previous, current = (current, advanced)
    later_adjoint = adjoint_prev
    adjoint = adjoint_now
    image_horizontal = jnp.zeros(grid_dims, jnp.float32)
    image_vertical = jnp.zeros(grid_dims, jnp.float32)
    for time_step in range(STEPS - 1, -1, -1):
        horizontal, vertical = curvatures(adjoint_rims_of(adjoint))
        wave_horizontal = saved_first[time_step]
        wave_vertical = saved_second[time_step]
        earlier = 2.0 * adjoint - later_adjoint + speeds * (hfactor * horizontal + vertical)
        spread = jnp.where(lane_hot, misfits[time_step][:, None], 0.0)
        injected = select_dot(row_hot.T, spread)
        earlier = earlier + injected.reshape(grid_dims)
        image_horizontal = image_horizontal + earlier * wave_horizontal
        image_vertical = image_vertical + earlier * wave_vertical
        later_adjoint, adjoint = (adjoint, earlier)
    gradient_speed = hfactor * image_horizontal + image_vertical
    gradient_aniso = 2.0 * speeds * image_horizontal
    stacked = jnp.stack([gradient_speed, gradient_aniso, speeds], axis=1)
    widened = image_rims_of(stacked)
    me = lax.axis_index("shot")
    position = (me + SPLIT // 2) % SPLIT
    layer = lax.broadcasted_iota(jnp.int32, (1, 1, widened.shape[2], 1), 2)
    has_below = jnp.logical_and(position > 0, me > 0)
    has_above = jnp.logical_and(position < SPLIT - 1, me < shot_count - 1)
    exists = jnp.where(layer == 0, has_below, jnp.where(layer == widened.shape[2] - 1, has_above, True))
    ones = jnp.broadcast_to(exists.astype(jnp.float32), widened[:, :1].shape)
    smoothed = diffuse(jnp.concatenate([widened, ones], axis=1))
    rows_out = smoothed.reshape(NEED, 2 * row_len)
    returning = jnp.dot(place_hot.T, rows_out, precision=lax.Precision.HIGHEST)
    returned = lax.all_to_all(
        returning.reshape(shot_count, capacity, 2 * row_len),
        "shot",
        split_axis=0,
        concat_axis=0,
        tiled=True,
    ).reshape(slots_all, 2 * row_len)
    summed = jnp.dot(pick.T, returned, precision=lax.Precision.HIGHEST)
    return (current, (summed * IMAGE_GAIN).reshape(owned, 2, row_len))


def solution(mesh):
    placed = (
        P(("groups", "shot"), None),
        P(("groups", "shot"), None),
        P(("groups", "shot"), None),
        P(("groups", "shot")),
        P(("groups", "shot"), None, None),
        P(("groups", "shot"), None, None),
        P(("groups", "shot"), None, None),
        P(("groups", "shot"), None, None),
        P(("groups", "shot")),
        P(("groups", "shot"), None),
        P(("groups", "shot"), None),
        P(("groups", "shot"), None, None),
    )
    return jax.shard_map(
        shards,
        mesh=mesh,
        in_specs=placed,
        out_specs=(P(("groups", "shot"), None, None), P(("groups", "shot"), None, None)),
        check_vma=False,
    )
```
